256 devices in a mesh: gx: 8 (over y, core), gy: 4 (over z_hi), gz: 8 (over x, z_lo).
Axes of the slice: x: 4, y: 4, z: 8 (z_hi: 4, z_lo: 2; z = z_hi * 2 + z_lo), core: 2. Of those that a mesh axis runs over, the one named last changes fastest.
Arguments:
- scalars: float32 [8, 4, 8, 128, 128], P('gx', 'gy', 'gz'), may hold values from -6 to 6
- vectors: float32 [8, 4, 8, 3, 128, 128], P('gx', 'gy', 'gz'), may hold values from -6 to 6
- positions: float32 [8, 4, 8, 3, 128], P('gx', 'gy', 'gz'), may hold values from 0 to 6
- species: int32 [8, 4, 8, 128], P('gx', 'gy', 'gz'), may hold values from 0 to 7
- atom_count: int32 [8, 4, 8], P('gx', 'gy', 'gz'), may hold values from 64 to 128, as said below
- energy_weight: float32 [8, 4, 8, 128], P('gx', 'gy', 'gz'), may hold values from -5 to 5
- local_pairs: int32 [8, 4, 8, 2, 1024], P('gx', 'gy', 'gz'), may hold values from 0 to 127, as said below
- face_pairs: int32 [8, 4, 8, 3, 2, 256], P('gx', 'gy', 'gz'), may hold values from 0 to 127, as said below
- tile_counts: int32 [8, 4, 8, 4], P('gx', 'gy', 'gz'), may hold values from 85 to 1024, as said below
- w_center: float32 [128, 128], replicated, may hold values from -0.5 to 0.5
- w_partner: float32 [128, 128], replicated, may hold values from -0.5 to 0.5
- w_radial: float32 [8, 128], replicated, may hold values from -4 to 4
- species_embed: float32 [2, 8, 128], replicated, may hold values from -3 to 3
- w_mix: float32 [128, 128], replicated, may hold values from -0.5 to 0.5
- w_channel: float32 [2, 128, 128], replicated, may hold values from -0.5 to 0.5
- w_read: float32 [128, 128], replicated, may hold values from -0.5 to 0.5
- w_out: float32 [128], replicated, may hold values from -0.5 to 0.5
- species_energy: float32 [8], replicated, may hold values from -2 to 2
Outputs:
- atom_energy: float32 [8, 4, 8, 128], P('gx', 'gy', 'gz')
- position_grad: float32 [8, 4, 8, 3, 128], P('gx', 'gy', 'gz')
- scalar_grad: float32 [8, 4, 8, 128, 128], P('gx', 'gy', 'gz')
- vector_grad: float32 [8, 4, 8, 3, 128, 128], P('gx', 'gy', 'gz')
- weight_grad: float32 [101512], replicated
The draws below stay inside these ranges and needn't reach their ends.
Inputs may be any that keep to these rules, and one draw needn't show every extreme that they name: `atom_count`: some domain holds exactly 128 live atoms; slots at or above a domain's count are padding. `tile_counts`: entry 0 counts the live slots of the local tile (at least 512), entries 1 to 3 those of the face tiles (at least 85); some domain fills all four tiles. `local_pairs`: every slot names two different atoms of the domain, both below its atom count; live slots are those below tile_counts[0]. `face_pairs`: in tile d, entry 0 names an atom below this domain's count and entry 1 an atom below the count of the next domain along grid direction d (wrapping around); live slots are those below tile_counts[1 + d].
All inputs are finite; a program needn't handle non-finite values.
Results may differ from the reference program's by a relative error of at most 0.0003.
Values sent between devices are 32-bit elements; how exact they have to be, the bound alone decides.
No kernel may reach another device: no remote copies, remote signals or barrier semaphores. Data moves between devices by JAX's collectives and lax.ppermute only.
A program may use at most 128 MiB of HBM per device.

```python
import jax
import jax.numpy as jnp
from jax import lax

CHANNELS = 128
BASIS = 8
SPECIES = 8
ATOMS_DEV = 128
DOM_X = 8
DOM_Y = 4
DOM_Z = 8
LOCAL_PAIRS = 1024
FACE_PAIRS = 256


def pair_tables(key):
    domain_shape = (DOM_X, DOM_Y, DOM_Z)
    domain_total = DOM_X * DOM_Y * DOM_Z
    atom_counts = jax.random.randint(jax.random.fold_in(key, 101), domain_shape, ATOMS_DEV // 2, ATOMS_DEV + 1)
    fullest = jax.random.randint(jax.random.fold_in(key, 102), (), 0, domain_total)
    marker = (jnp.arange(domain_total) == fullest).reshape(domain_shape)
    atom_counts = jnp.where(marker, ATOMS_DEV, atom_counts).astype(jnp.int32)
    local_live = jax.random.randint(jax.random.fold_in(key, 103), domain_shape, LOCAL_PAIRS // 2, LOCAL_PAIRS + 1)
    face_live = jax.random.randint(jax.random.fold_in(key, 104), domain_shape + (3,), FACE_PAIRS // 3, FACE_PAIRS + 1)
    local_live = jnp.where(marker, LOCAL_PAIRS, local_live)
    face_live = jnp.where(marker[..., None], FACE_PAIRS, face_live)
    tile_totals = jnp.concatenate([local_live[..., None], face_live], axis=-1).astype(jnp.int32)
    upper_limit = atom_counts[..., None]
    center_atoms = jax.random.randint(jax.random.fold_in(key, 105), domain_shape + (LOCAL_PAIRS,), 0, upper_limit)
    step_sizes = jax.random.randint(jax.random.fold_in(key, 106), domain_shape + (LOCAL_PAIRS,), 1, upper_limit)
    partner_atoms = (center_atoms + step_sizes) % upper_limit
    local_table = jnp.stack([center_atoms, partner_atoms], axis=3).astype(jnp.int32)
    face_tables = []
    for direction in range(3):
        neighbour_counts = jnp.roll(atom_counts, -1, axis=direction)[..., None]
        near_atoms = jax.random.randint(jax.random.fold_in(key, 107 + 2 * direction), domain_shape + (FACE_PAIRS,), 0, upper_limit)
        far_atoms = jax.random.randint(jax.random.fold_in(key, 108 + 2 * direction), domain_shape + (FACE_PAIRS,), 0, neighbour_counts)
        face_tables.append(jnp.stack([near_atoms, far_atoms], axis=3))
    face_table = jnp.stack(face_tables, axis=3).astype(jnp.int32)
    return (atom_counts, tile_totals, local_table, face_table)


def draw_atom_count(key, part):
    return pair_tables(key)[0]


def draw_tile_counts(key, part):
    return pair_tables(key)[1]


def draw_local_pairs(key, part):
    return pair_tables(key)[2]


def draw_face_pairs(key, part):
    return pair_tables(key)[3]


def set_ends(values, own_key, smallest, largest):
    longest = values.shape.index(max(values.shape))
    spots = []
    for shift in (0, 1):
        where = [jax.random.randint(jax.random.fold_in(own_key, axis), (), 0, length) for axis, length in enumerate(values.shape)]
        where[longest] = (where[longest] + shift) % values.shape[longest]
        spots.append(tuple(where))
    return values.at[spots[0]].set(smallest).at[spots[1]].set(largest)


def block_scale(key, shape, cuts, least, top_value):
    factor_of = 1.0
    for position, shards_of in cuts:
        draws = jax.random.uniform(jax.random.fold_in(jax.random.fold_in(key, 6), position), (shards_of,), jnp.float32, least / len(cuts), top_value / len(cuts))
        factor_of = factor_of * jnp.repeat(jnp.exp(draws), shape[position] // shards_of).reshape((-1,) + (1,) * (len(shape) - 1 - position))
    return factor_of


def gaussian(rng, dims, deviation, limit, pieces=(), kind=jnp.bfloat16):
    result = deviation * jax.random.normal(rng, dims, jnp.float32)
    if pieces:
        result = result * block_scale(rng, dims, pieces, -0.22, 0.18)
    return jnp.clip(result, -limit, limit).astype(kind)


def setup_inputs(seed: int = 0) -> dict:
    key_list = jax.random.split(jax.random.key(seed), 19)
    scalars = gaussian(key_list[0], (DOM_X, DOM_Y, DOM_Z, CHANNELS, ATOMS_DEV), 1.0, 6.0, ((0, 8), (1, 4), (2, 8)), jnp.float32)
    vectors = gaussian(key_list[1], (DOM_X, DOM_Y, DOM_Z, 3, CHANNELS, ATOMS_DEV), 1.0, 6.0, ((0, 8), (1, 4), (2, 8)), jnp.float32)
    positions = jnp.clip(6.0 * jax.random.uniform(key_list[2], (DOM_X, DOM_Y, DOM_Z, 3, ATOMS_DEV), jnp.float32) ** block_scale(key_list[2], (DOM_X, DOM_Y, DOM_Z, 3, ATOMS_DEV), ((0, 8), (1, 4), (2, 8)), -0.2, 0.2), 0.0, 6.0)
    species = set_ends(jax.random.randint(key_list[3], (DOM_X, DOM_Y, DOM_Z, ATOMS_DEV), 0, SPECIES), jax.random.fold_in(key_list[3], 1), 0, SPECIES - 1).astype(jnp.int32)
    atom_count = draw_atom_count(jax.random.fold_in(key_list[18], 71), 0)
    energy_weight = gaussian(key_list[5], (DOM_X, DOM_Y, DOM_Z, ATOMS_DEV), 1.0, 5.0, ((0, 8), (1, 4), (2, 8)), jnp.float32)
    local_pairs = draw_local_pairs(jax.random.fold_in(key_list[18], 71), 0)
    face_pairs = draw_face_pairs(jax.random.fold_in(key_list[18], 71), 0)
    tile_counts = draw_tile_counts(jax.random.fold_in(key_list[18], 71), 0)
    w_center = gaussian(key_list[9], (CHANNELS, CHANNELS), CHANNELS ** -0.5, 0.5, (), jnp.float32)
    w_partner = gaussian(key_list[10], (CHANNELS, CHANNELS), CHANNELS ** -0.5, 0.5, (), jnp.float32)
    w_radial = gaussian(key_list[11], (BASIS, CHANNELS), 0.8, 4.0, (), jnp.float32)
    species_embed = gaussian(key_list[12], (2, SPECIES, CHANNELS), 0.6, 3.0, (), jnp.float32)
    w_mix = gaussian(key_list[13], (CHANNELS, CHANNELS), CHANNELS ** -0.5, 0.5, (), jnp.float32)
    w_channel = gaussian(key_list[14], (2, CHANNELS, CHANNELS), CHANNELS ** -0.5, 0.5, (), jnp.float32)
    w_read = gaussian(key_list[15], (CHANNELS, CHANNELS), CHANNELS ** -0.5, 0.5, (), jnp.float32)
    w_out = gaussian(key_list[16], (CHANNELS,), CHANNELS ** -0.5, 0.5, (), jnp.float32)
    species_energy = jnp.clip(jax.random.uniform(key_list[17], (SPECIES,), jnp.float32, -2.0, 2.0), -2.0, 2.0)
    return dict(scalars=scalars, vectors=vectors, positions=positions, species=species, atom_count=atom_count, energy_weight=energy_weight, local_pairs=local_pairs, face_pairs=face_pairs, tile_counts=tile_counts, w_center=w_center, w_partner=w_partner, w_radial=w_radial, species_embed=species_embed, w_mix=w_mix, w_channel=w_channel, w_read=w_read, w_out=w_out, species_energy=species_energy)


cutoff_radius = 5.0
cell_edge = 6.0
highest = lax.Precision.HIGHEST

def edge_energy(edge_params, center_proj, partner_proj, center_vecs, partner_vecs, displace):
    radial_weight, mix_weight, channel_weight, read_weight, out_weight = edge_params
    squared = lax.optimization_barrier(jnp.sum(displace * displace, axis=0))
    basis_count = radial_weight.shape[0]
    spacing = cutoff_radius * cutoff_radius / (basis_count - 1)
    centers_sq = spacing * jnp.arange(basis_count).astype(jnp.float32)
    radial_basis = jnp.exp(-jnp.square((squared[None, :] - centers_sq[:, None]) / spacing))
    latent_in = center_proj + partner_proj + jnp.dot(radial_weight.T, radial_basis, precision=highest)
    first_hidden = jax.nn.silu(latent_in)
    second = first_hidden + jax.nn.silu(jnp.dot(mix_weight.T, first_hidden, precision=highest))
    vector_gain = jnp.dot(channel_weight[0].T, second, precision=highest)
    tensor_gain = jnp.dot(channel_weight[1].T, second, precision=highest)
    bond_vector = displace / cutoff_radius
    along_partner = lax.optimization_barrier(jnp.sum(bond_vector[:, None, :] * partner_vecs, axis=0))
    along_center = lax.optimization_barrier(jnp.sum(bond_vector[:, None, :] * center_vecs, axis=0))
    inner_product = lax.optimization_barrier(jnp.sum(center_vecs * partner_vecs, axis=0))
    scaled_sq = squared / (cutoff_radius * cutoff_radius)
    quadratic = along_center * along_partner - scaled_sq[None, :] * inner_product / 3.0
    mixed_latent = second + vector_gain * along_partner + tensor_gain * quadratic
    readout = jnp.dot(out_weight, jax.nn.silu(jnp.dot(read_weight.T, mixed_latent, precision=highest)), precision=highest)
    envelope = 1.0 / (1.0 + scaled_sq)
    return envelope * readout

def tile_loss(edge_params, center, partner, center_weight, partner_weight, pair_list, live_count, offset):
    center_proj, center_vecs, center_coords = center
    partner_proj, partner_vecs, partner_coords = partner
    center_rows = pair_list[0]
    partner_rows = pair_list[1]
    slot_count = pair_list.shape[1]
    live_mask = (jnp.arange(slot_count, dtype=jnp.int32) < live_count).astype(jnp.float32)
    displace = jnp.take(partner_coords, partner_rows, axis=1) + offset[:, None] - jnp.take(center_coords, center_rows, axis=1)
    energies = edge_energy(edge_params, jnp.take(center_proj, center_rows, axis=1), jnp.take(partner_proj, partner_rows, axis=1), jnp.take(center_vecs, center_rows, axis=2), jnp.take(partner_vecs, partner_rows, axis=2), displace)
    halves = 0.5 * live_mask * energies
    weighted_sum = jnp.sum(halves * (center_weight[center_rows] + partner_weight[partner_rows]))
    center_energy = jnp.zeros((center_proj.shape[1],), jnp.float32).at[center_rows].add(halves)
    partner_energy = jnp.zeros((partner_proj.shape[1],), jnp.float32).at[partner_rows].add(halves)
    return (weighted_sum, (center_energy, partner_energy))

def face_offset(direction):
    return cell_edge * (jnp.arange(3) == direction).astype(jnp.float32)

def domain_step(edge_params, domain_item):
    center_here, partner_here, vecs_here, coords_here, weights_here, local_list, face_list, live_counts, near_proj, near_vecs, near_coords, near_weights = domain_item
    center = (center_here, vecs_here, coords_here)
    weighted_sum, (center_energy, partner_energy) = tile_loss(edge_params, center, (partner_here, vecs_here, coords_here), weights_here, weights_here, local_list, live_counts[0], jnp.zeros((3,), jnp.float32))
    pair_energy = center_energy + partner_energy
    returned = []
    for direction in range(3):
        face_sum, (center_face, partner_face) = tile_loss(edge_params, center, (near_proj[direction], near_vecs[direction], near_coords[direction]), weights_here, near_weights[direction], face_list[direction], live_counts[direction + 1], face_offset(direction))
        weighted_sum = weighted_sum + face_sum
        pair_energy = pair_energy + center_face
        returned.append(partner_face)
    return (weighted_sum, pair_energy, jnp.stack(returned, axis=0))

def reference(scalars, vectors, positions, species, atom_count, energy_weight, local_pairs, face_pairs, tile_counts, w_center, w_partner, w_radial, species_embed, w_mix, w_channel, w_read, w_out, species_energy):
    grid_shape = scalars.shape[:3]
    domain_total = grid_shape[0] * grid_shape[1] * grid_shape[2]
    atom_slots = scalars.shape[4]
    kind_count = species_energy.shape[0]
    species_hot = (species[..., None, :] == jnp.arange(kind_count, dtype=jnp.int32)[:, None]).astype(jnp.float32)
    valid_atoms = (jnp.arange(atom_slots, dtype=jnp.int32) < atom_count[..., None]).astype(jnp.float32)

    def flat_domains(array):
        return array.reshape((domain_total,) + array.shape[3:])

    def neighbours(array):
        return flat_domains(jnp.stack([jnp.roll(array, -1, axis=direction) for direction in range(3)], axis=3))
    checked_step = jax.checkpoint(domain_step)

    def total_loss(center_matrix, partner_matrix, radial_matrix, embed_table, mix_matrix, channel_matrix, read_matrix, out_vector, reference_energy, scalar_in, vector_in, coords_in):
        center_proj = jnp.einsum('dc,xyzda->xyzca', center_matrix, scalar_in, precision=highest) + jnp.einsum('sc,xyzsa->xyzca', embed_table[0], species_hot, precision=highest)
        partner_proj = jnp.einsum('dc,xyzda->xyzca', partner_matrix, scalar_in, precision=highest) + jnp.einsum('sc,xyzsa->xyzca', embed_table[1], species_hot, precision=highest)
        self_energy = valid_atoms * jnp.einsum('s,xyzsa->xyza', reference_energy, species_hot, precision=highest)
        edge_params = (radial_matrix, mix_matrix, channel_matrix, read_matrix, out_vector)
        domain_items = (flat_domains(center_proj), flat_domains(partner_proj), flat_domains(vector_in), flat_domains(coords_in), flat_domains(energy_weight), flat_domains(local_pairs), flat_domains(face_pairs), flat_domains(tile_counts), neighbours(partner_proj), neighbours(vector_in), neighbours(coords_in), neighbours(energy_weight))
        losses, pair_energy, returned = lax.map(lambda domain_item: checked_step(edge_params, domain_item), domain_items)
        pair_energy = pair_energy.reshape(grid_shape + (atom_slots,))
        returned = returned.reshape(grid_shape + (3, atom_slots))
        for direction in range(3):
            pair_energy = pair_energy + jnp.roll(returned[..., direction, :], 1, axis=direction)
        atom_energy = self_energy + pair_energy
        return (jnp.sum(losses) + jnp.sum(energy_weight * self_energy), atom_energy)
    primal, pull_back, atom_energy = jax.vjp(total_loss, w_center, w_partner, w_radial, species_embed, w_mix, w_channel, w_read, w_out, species_energy, scalars, vectors, positions, has_aux=True)
    grads = pull_back(jnp.ones_like(primal))
    weight_grad = jnp.concatenate([piece_grad.reshape(-1) for piece_grad in grads[:9]]) / domain_total
    return (atom_energy, grads[11], grads[9], grads[10], weight_grad)
```

```python
import jax
import jax.numpy as jnp
from jax import lax
from jax.sharding import PartitionSpec as P

cutoff_radius = 5.0
cell_edge = 6.0
highest = lax.Precision.HIGHEST


def from_behind(block, axis, distance):
    devices = range(lax.axis_size(axis))
    route = [((i - distance) % len(devices), i) for i in devices]
    return lax.ppermute(block, axis, route)


def edge_energy(edge_params, center_proj, partner_proj, center_vecs, partner_vecs, displace):
    radial_weight, mix_weight, channel_weight, read_weight, out_weight = edge_params
    squared = jnp.sum(displace * displace, axis=0)
    basis_count = radial_weight.shape[0]
    spacing = cutoff_radius * cutoff_radius / (basis_count - 1)
    centers_sq = spacing * jnp.arange(basis_count).astype(jnp.float32)
    radial_basis = jnp.exp(-jnp.square((squared[None, :] - centers_sq[:, None]) / spacing))
    latent_in = (
        center_proj + partner_proj + jnp.dot(radial_weight.T, radial_basis, precision=highest)
    )
    first_hidden = jax.nn.silu(latent_in)
    second = first_hidden + jax.nn.silu(jnp.dot(mix_weight.T, first_hidden, precision=highest))
    vector_gain = jnp.dot(channel_weight[0].T, second, precision=highest)
    tensor_gain = jnp.dot(channel_weight[1].T, second, precision=highest)
    bond_vector = displace / cutoff_radius
    along_partner = jnp.sum(bond_vector[:, None, :] * partner_vecs, axis=0)
    along_center = jnp.sum(bond_vector[:, None, :] * center_vecs, axis=0)
    inner_product = jnp.sum(center_vecs * partner_vecs, axis=0)
    scaled_sq = squared / (cutoff_radius * cutoff_radius)
    quadratic = along_center * along_partner - scaled_sq[None, :] * inner_product / 3.0
    mixed_latent = second + vector_gain * along_partner + tensor_gain * quadratic
    readout = jnp.dot(
        out_weight,
        jax.nn.silu(jnp.dot(read_weight.T, mixed_latent, precision=highest)),
        precision=highest,
    )
    envelope = 1.0 / (1.0 + scaled_sq)
    return envelope * readout


def shift(payload, direction, distance):
    return from_behind(payload, ("gx", "gy", "gz")[direction], distance)


def halving_steps():
    steps = []
    for axis in ("gx", "gz", "gy"):
        size = lax.axis_size(axis)
        distance = 1
        while distance < size:
            steps.append((axis, distance, size))
            distance *= 2
    return steps


def sum_over_devices(flat):
    steps = halving_steps()
    if any(size & (size - 1) for _, _, size in steps):
        return lax.psum(flat, ("gx", "gy", "gz"))
    pieces = 2 ** len(steps)
    padded = jnp.pad(flat, (0, (-flat.shape[0]) % pieces))
    for axis, distance, size in steps:
        upper = (lax.axis_index(axis) // distance) % 2 == 1
        half = padded.shape[0] // 2
        low, high = padded[:half], padded[half:]
        keep = jnp.where(upper, high, low)
        send = jnp.where(upper, low, high)
        padded = keep + lax.ppermute(send, axis, [(i, i ^ distance) for i in range(size)])
    for axis, distance, size in reversed(steps):
        upper = (lax.axis_index(axis) // distance) % 2 == 1
        other = lax.ppermute(padded, axis, [(i, i ^ distance) for i in range(size)])
        padded = jnp.where(
            upper, jnp.concatenate([other, padded]), jnp.concatenate([padded, other])
        )
    return padded[: flat.shape[0]]


def one_hot(rows, slots):
    return (jnp.arange(slots, dtype=jnp.int32)[:, None] == rows[None, :]).astype(jnp.float32)


def per_device(
    scalars,
    vectors,
    positions,
    species,
    atom_count,
    energy_weight,
    local_pairs,
    face_pairs,
    tile_counts,
    w_center,
    w_partner,
    w_radial,
    species_embed,
    w_mix,
    w_channel,
    w_read,
    w_out,
    species_energy,
):
    scalar_in = scalars[0, 0, 0]
    vector_in = vectors[0, 0, 0]
    coords = positions[0, 0, 0]
    weights_here = energy_weight[0, 0, 0]
    live_counts = tile_counts[0, 0, 0]
    local_list = local_pairs[0, 0, 0]
    face_list = face_pairs[0, 0, 0]
    channels, atom_slots = scalar_in.shape
    vector_rows = 3 * channels
    table_rows = channels + vector_rows + 3
    kind_count = species_energy.shape[0]
    local_slots = local_list.shape[1]
    face_slots = face_list.shape[2]
    species_hot = (
        species[0, 0, 0][None, :] == jnp.arange(kind_count, dtype=jnp.int32)[:, None]
    ).astype(jnp.float32)
    valid_atoms = (jnp.arange(atom_slots, dtype=jnp.int32) < atom_count[0, 0, 0]).astype(
        jnp.float32
    )

    def atom_side(center_matrix, partner_matrix, embed_table, features):
        center_proj = jnp.dot(center_matrix.T, features, precision=highest) + jnp.dot(
            embed_table[0].T, species_hot, precision=highest
        )
        partner_proj = jnp.dot(partner_matrix.T, features, precision=highest) + jnp.dot(
            embed_table[1].T, species_hot, precision=highest
        )
        return (center_proj, partner_proj)

    (center_proj, partner_proj), atom_back = jax.vjp(
        atom_side, w_center, w_partner, species_embed, scalar_in
    )
    edge_params = (w_radial, w_mix, w_channel, w_read, w_out)
    vector_flat = vector_in.reshape(vector_rows, atom_slots)
    center_table = jnp.concatenate([center_proj, vector_flat, coords], axis=0)
    packet = jnp.concatenate([partner_proj, vector_flat, coords, weights_here[None, :]], axis=0)
    arrived = [shift(packet, direction, -1) for direction in range(3)]
    partner_tables = [packet[:table_rows]] + [incoming[:table_rows] for incoming in arrived]
    partner_weights = [weights_here] + [incoming[table_rows] for incoming in arrived]

    center_rows = jnp.concatenate([local_list[0]] + [face_list[d, 0] for d in range(3)])
    partner_rows = [local_list[1]] + [face_list[d, 1] for d in range(3)]
    center_hot = one_hot(center_rows, atom_slots)
    partner_hot = [one_hot(rows, atom_slots) for rows in partner_rows]
    slot_sizes = [local_slots] + [face_slots] * 3
    live_mask = jnp.concatenate(
        [
            (jnp.arange(size, dtype=jnp.int32) < live_counts[tile]).astype(jnp.float32)
            for tile, size in enumerate(slot_sizes)
        ]
    )
    offset = jnp.concatenate(
        [jnp.zeros((3, local_slots), jnp.float32)]
        + [
            jnp.broadcast_to(
                cell_edge * (jnp.arange(3) == d).astype(jnp.float32)[:, None], (3, face_slots)
            )
            for d in range(3)
        ],
        axis=1,
    )
    pair_weight = jnp.dot(weights_here, center_hot, precision=highest) + jnp.concatenate(
        [
            jnp.dot(weight_row, hot, precision=highest)
            for weight_row, hot in zip(partner_weights, partner_hot)
        ]
    )

    def pair_loss(params_in, center_in, partner_in):
        center_side = jnp.dot(center_in, center_hot, precision=highest)
        partner_side = jnp.concatenate(
            [jnp.dot(table, hot, precision=highest) for table, hot in zip(partner_in, partner_hot)],
            axis=1,
        )
        pair_count = center_side.shape[1]
        displace = partner_side[channels + vector_rows :] + offset - center_side[channels + vector_rows :]
        energies = edge_energy(
            params_in,
            center_side[:channels],
            partner_side[:channels],
            center_side[channels : channels + vector_rows].reshape(3, channels, pair_count),
            partner_side[channels : channels + vector_rows].reshape(3, channels, pair_count),
            displace,
        )
        halves = 0.5 * live_mask * energies
        return jnp.sum(halves * pair_weight), halves

    weighted_sum, pull_back, halves = jax.vjp(
        pair_loss, edge_params, center_table, partner_tables, has_aux=True
    )
    param_grad, center_grad, partner_grad = pull_back(jnp.ones_like(weighted_sum))
    center_energy = jnp.dot(center_hot, halves, precision=highest)
    starts = [0, local_slots] + [local_slots + face_slots * (d + 1) for d in range(3)]
    partner_energy = [
        jnp.dot(hot, halves[starts[tile] : starts[tile + 1]], precision=highest)
        for tile, hot in enumerate(partner_hot)
    ]

    returned = [
        shift(
            jnp.concatenate([partner_grad[d + 1], partner_energy[d + 1][None, :]], axis=0),
            d,
            1,
        )
        for d in range(3)
    ]
    table_grad = center_grad + partner_grad[0]
    for back_in in returned:
        table_grad = table_grad + back_in[:table_rows]
    pair_energy = center_energy + partner_energy[0]
    for back_in in returned:
        pair_energy = pair_energy + back_in[table_rows]
    center_proj_grad = center_grad[:channels]
    partner_proj_grad = partner_grad[0][:channels]
    for back_in in returned:
        partner_proj_grad = partner_proj_grad + back_in[:channels]
    vector_grad = table_grad[channels : channels + vector_rows].reshape(3, channels, atom_slots)
    coord_grad = table_grad[channels + vector_rows :]

    center_matrix_grad, partner_matrix_grad, embed_grad, scalar_grad = atom_back(
        (center_proj_grad, partner_proj_grad)
    )
    self_energy = valid_atoms * jnp.dot(species_energy, species_hot, precision=highest)
    reference_grad = jnp.dot(species_hot, weights_here * valid_atoms, precision=highest)
    local_flat = jnp.concatenate(
        [
            center_matrix_grad.reshape(-1),
            partner_matrix_grad.reshape(-1),
            param_grad[0].reshape(-1),
            embed_grad.reshape(-1),
            param_grad[1].reshape(-1),
            param_grad[2].reshape(-1),
            param_grad[3].reshape(-1),
            param_grad[4].reshape(-1),
            reference_grad,
        ]
    )
    domain_total = lax.axis_size("gx") * lax.axis_size("gy") * lax.axis_size("gz")
    summed = sum_over_devices(local_flat)
    weight_grad = summed / domain_total
    atom_energy = self_energy + pair_energy
    return (
        atom_energy[None, None, None],
        coord_grad[None, None, None],
        scalar_grad[None, None, None],
        vector_grad[None, None, None],
        weight_grad,
    )


def solution(mesh):
    return jax.shard_map(
        per_device,
        mesh=mesh,
        in_specs=(
            P("gx", "gy", "gz", None, None),
            P("gx", "gy", "gz", None, None, None),
            P("gx", "gy", "gz", None, None),
            P("gx", "gy", "gz", None),
            P("gx", "gy", "gz"),
            P("gx", "gy", "gz", None),
            P("gx", "gy", "gz", None, None),
            P("gx", "gy", "gz", None, None, None),
            P("gx", "gy", "gz", None),
            P(),
            P(),
            P(),
            P(),
            P(),
            P(),
            P(),
            P(),
            P(),
        ),
        out_specs=(
            P("gx", "gy", "gz", None),
            P("gx", "gy", "gz", None, None),
            P("gx", "gy", "gz", None, None),
            P("gx", "gy", "gz", None, None, None),
            P(),
        ),
        check_vma=False,
    )
```

```python
import jax
import jax.numpy as jnp
from jax import lax
from jax.sharding import PartitionSpec as P

cutoff_radius = 5.0
cell_edge = 6.0
highest = lax.Precision.HIGHEST


def from_behind(block, axis, distance):
    devices = range(lax.axis_size(axis))
    route = [((i - distance) % len(devices), i) for i in devices]
    return lax.ppermute(block, axis, route)


def edge_energy(edge_params, center_proj, partner_proj, center_vecs, partner_vecs, displace):
    radial_weight, mix_weight, channel_weight, read_weight, out_weight = edge_params
    squared = jnp.sum(displace * displace, axis=0)
    basis_count = radial_weight.shape[0]
    spacing = cutoff_radius * cutoff_radius / (basis_count - 1)
    centers_sq = spacing * jnp.arange(basis_count).astype(jnp.float32)
    radial_basis = jnp.exp(-jnp.square((squared[None, :] - centers_sq[:, None]) / spacing))
    latent_in = (
        center_proj + partner_proj + jnp.dot(radial_weight.T, radial_basis, precision=highest)
    )
    first_hidden = jax.nn.silu(latent_in)
    second = first_hidden + jax.nn.silu(jnp.dot(mix_weight.T, first_hidden, precision=highest))
    vector_gain = jnp.dot(channel_weight[0].T, second, precision=highest)
    tensor_gain = jnp.dot(channel_weight[1].T, second, precision=highest)
    bond_vector = displace / cutoff_radius
    along_partner = jnp.sum(bond_vector[:, None, :] * partner_vecs, axis=0)
    along_center = jnp.sum(bond_vector[:, None, :] * center_vecs, axis=0)
    inner_product = jnp.sum(center_vecs * partner_vecs, axis=0)
    scaled_sq = squared / (cutoff_radius * cutoff_radius)
    quadratic = along_center * along_partner - scaled_sq[None, :] * inner_product / 3.0
    mixed_latent = second + vector_gain * along_partner + tensor_gain * quadratic
    readout = jnp.dot(
        out_weight,
        jax.nn.silu(jnp.dot(read_weight.T, mixed_latent, precision=highest)),
        precision=highest,
    )
    envelope = 1.0 / (1.0 + scaled_sq)
    return envelope * readout


def shift(payload, direction, distance):
    return from_behind(payload, ("gx", "gy", "gz")[direction], distance)


def halving_steps():
    steps = []
    for axis in ("gx", "gz", "gy"):
        size = lax.axis_size(axis)
        distance = 1
        while distance < size:
            steps.append((axis, distance, size))
            distance *= 2
    return steps


def sum_over_devices(flat):
    steps = halving_steps()
    if any(size & (size - 1) for _, _, size in steps):
        return lax.psum(flat, ("gx", "gy", "gz"))
    pieces = 2 ** len(steps)
    padded = jnp.pad(flat, (0, (-flat.shape[0]) % pieces))
    for axis, distance, size in steps:
        upper = (lax.axis_index(axis) // distance) % 2 == 1
        half = padded.shape[0] // 2
        low, high = padded[:half], padded[half:]
        keep = jnp.where(upper, high, low)
        send = jnp.where(upper, low, high)
        padded = keep + lax.ppermute(send, axis, [(i, i ^ distance) for i in range(size)])
    for axis, distance, size in reversed(steps):
        upper = (lax.axis_index(axis) // distance) % 2 == 1
        other = lax.ppermute(padded, axis, [(i, i ^ distance) for i in range(size)])
        padded = jnp.where(
            upper, jnp.concatenate([other, padded]), jnp.concatenate([padded, other])
        )
    return padded[: flat.shape[0]]


def one_hot(rows, slots):
    return (jnp.arange(slots, dtype=jnp.int32)[:, None] == rows[None, :]).astype(jnp.float32)


def per_device(
    scalars,
    vectors,
    positions,
    species,
    atom_count,
    energy_weight,
    local_pairs,
    face_pairs,
    tile_counts,
    w_center,
    w_partner,
    w_radial,
    species_embed,
    w_mix,
    w_channel,
    w_read,
    w_out,
    species_energy,
):
    scalar_in = scalars[0, 0, 0]
    vector_in = vectors[0, 0, 0]
    coords = positions[0, 0, 0]
    weights_here = energy_weight[0, 0, 0]
    live_counts = tile_counts[0, 0, 0]
    local_list = local_pairs[0, 0, 0]
    face_list = face_pairs[0, 0, 0]
    channels, atom_slots = scalar_in.shape
    vector_rows = 3 * channels
    table_rows = channels + vector_rows + 3
    kind_count = species_energy.shape[0]
    local_slots = local_list.shape[1]
    face_slots = face_list.shape[2]
    species_hot = (
        species[0, 0, 0][None, :] == jnp.arange(kind_count, dtype=jnp.int32)[:, None]
    ).astype(jnp.float32)
    valid_atoms = (jnp.arange(atom_slots, dtype=jnp.int32) < atom_count[0, 0, 0]).astype(
        jnp.float32
    )

    edge_params = (w_radial, w_mix, w_channel, w_read, w_out)
    vector_flat = vector_in.reshape(vector_rows, atom_slots)
    own_table = jnp.concatenate([scalar_in, vector_flat, coords], axis=0)
    species_row = species[0, 0, 0].astype(jnp.float32)
    packet = jnp.concatenate([own_table, weights_here[None, :], species_row[None, :]], axis=0)
    arrived = [shift(packet, direction, -1) for direction in range(3)]
    far_tables = [incoming[:table_rows] for incoming in arrived]
    partner_weights = [weights_here] + [incoming[table_rows] for incoming in arrived]
    partner_species = [species_hot] + [
        (incoming[table_rows + 1][None, :] == jnp.arange(kind_count, dtype=jnp.float32)[:, None]).astype(
            jnp.float32
        )
        for incoming in arrived
    ]

    center_rows = jnp.concatenate([local_list[0]] + [face_list[d, 0] for d in range(3)])
    partner_rows = [local_list[1]] + [face_list[d, 1] for d in range(3)]
    center_hot = one_hot(center_rows, atom_slots)
    partner_hot = [one_hot(rows, atom_slots) for rows in partner_rows]
    slot_sizes = [local_slots] + [face_slots] * 3
    live_mask = jnp.concatenate(
        [
            (jnp.arange(size, dtype=jnp.int32) < live_counts[tile]).astype(jnp.float32)
            for tile, size in enumerate(slot_sizes)
        ]
    )
    offset = jnp.concatenate(
        [jnp.zeros((3, local_slots), jnp.float32)]
        + [
            jnp.broadcast_to(
                cell_edge * (jnp.arange(3) == d).astype(jnp.float32)[:, None], (3, face_slots)
            )
            for d in range(3)
        ],
        axis=1,
    )
    pair_weight = jnp.dot(weights_here, center_hot, precision=highest) + jnp.concatenate(
        [
            jnp.dot(weight_row, hot, precision=highest)
            for weight_row, hot in zip(partner_weights, partner_hot)
        ]
    )

    def pair_loss(center_matrix, partner_matrix, embed_table, params_in, own_in, far_in):
        def projected(matrix, embed_row, table, hot_kinds):
            proj = jnp.dot(matrix.T, table[:channels], precision=highest) + jnp.dot(
                embed_row.T, hot_kinds, precision=highest
            )
            return jnp.concatenate([proj, table[channels:]], axis=0)

        center_in = projected(center_matrix, embed_table[0], own_in, species_hot)
        partner_in = [
            projected(partner_matrix, embed_table[1], table, hot_kinds)
            for table, hot_kinds in zip([own_in] + list(far_in), partner_species)
        ]
        center_side = jnp.dot(center_in, center_hot, precision=highest)
        partner_side = jnp.concatenate(
            [jnp.dot(table, hot, precision=highest) for table, hot in zip(partner_in, partner_hot)],
            axis=1,
        )
        pair_count = center_side.shape[1]
        displace = (
            partner_side[channels + vector_rows :] + offset - center_side[channels + vector_rows :]
        )
        energies = edge_energy(
            params_in,
            center_side[:channels],
            partner_side[:channels],
            center_side[channels : channels + vector_rows].reshape(3, channels, pair_count),
            partner_side[channels : channels + vector_rows].reshape(3, channels, pair_count),
            displace,
        )
        halves = 0.5 * live_mask * energies
        return jnp.sum(halves * pair_weight), halves

    weighted_sum, pull_back, halves = jax.vjp(
        pair_loss, w_center, w_partner, species_embed, edge_params, own_table, far_tables,
        has_aux=True,
    )
    center_matrix_grad, partner_matrix_grad, embed_grad, param_grad, own_grad, far_grad = pull_back(
        jnp.ones_like(weighted_sum)
    )
    center_energy = jnp.dot(center_hot, halves, precision=highest)
    starts = [0, local_slots] + [local_slots + face_slots * (d + 1) for d in range(3)]
    partner_energy = [
        jnp.dot(hot, halves[starts[tile] : starts[tile + 1]], precision=highest)
        for tile, hot in enumerate(partner_hot)
    ]

    returned = [
        shift(jnp.concatenate([far_grad[d], partner_energy[d + 1][None, :]], axis=0), d, 1)
        for d in range(3)
    ]
    table_grad = own_grad
    for back_in in returned:
        table_grad = table_grad + back_in[:table_rows]
    pair_energy = center_energy + partner_energy[0]
    for back_in in returned:
        pair_energy = pair_energy + back_in[table_rows]
    scalar_grad = table_grad[:channels]
    vector_grad = table_grad[channels : channels + vector_rows].reshape(3, channels, atom_slots)
    coord_grad = table_grad[channels + vector_rows :]

    self_energy = valid_atoms * jnp.dot(species_energy, species_hot, precision=highest)
    reference_grad = jnp.dot(species_hot, weights_here * valid_atoms, precision=highest)
    local_flat = jnp.concatenate(
        [
            center_matrix_grad.reshape(-1),
            partner_matrix_grad.reshape(-1),
            param_grad[0].reshape(-1),
            embed_grad.reshape(-1),
            param_grad[1].reshape(-1),
            param_grad[2].reshape(-1),
            param_grad[3].reshape(-1),
            param_grad[4].reshape(-1),
            reference_grad,
        ]
    )
    domain_total = lax.axis_size("gx") * lax.axis_size("gy") * lax.axis_size("gz")
    summed = sum_over_devices(local_flat)
    weight_grad = summed / domain_total
    atom_energy = self_energy + pair_energy
    return (
        atom_energy[None, None, None],
        coord_grad[None, None, None],
        scalar_grad[None, None, None],
        vector_grad[None, None, None],
        weight_grad,
    )


def solution(mesh):
    return jax.shard_map(
        per_device,
        mesh=mesh,
        in_specs=(
            P("gx", "gy", "gz", None, None),
            P("gx", "gy", "gz", None, None, None),
            P("gx", "gy", "gz", None, None),
            P("gx", "gy", "gz", None),
            P("gx", "gy", "gz"),
            P("gx", "gy", "gz", None),
            P("gx", "gy", "gz", None, None),
            P("gx", "gy", "gz", None, None, None),
            P("gx", "gy", "gz", None),
            P(),
            P(),
            P(),
            P(),
            P(),
            P(),
            P(),
            P(),
            P(),
        ),
        out_specs=(
            P("gx", "gy", "gz", None),
            P("gx", "gy", "gz", None, None),
            P("gx", "gy", "gz", None, None),
            P("gx", "gy", "gz", None, None, None),
            P(),
        ),
        check_vma=False,
    )
```

```python
import jax
import jax.numpy as jnp
from jax import lax
from jax.sharding import PartitionSpec as P

cutoff_radius = 5.0
cell_edge = 6.0
highest = lax.Precision.HIGHEST
halving_count = 3


def from_behind(block, axis, distance):
    devices = range(lax.axis_size(axis))
    route = [((i - distance) % len(devices), i) for i in devices]
    return lax.ppermute(block, axis, route)


def edge_energy(edge_params, center_proj, partner_proj, center_vecs, partner_vecs, displace):
    radial_weight, mix_weight, channel_weight, read_weight, out_weight = edge_params
    squared = jnp.sum(displace * displace, axis=0)
    basis_count = radial_weight.shape[0]
    spacing = cutoff_radius * cutoff_radius / (basis_count - 1)
    centers_sq = spacing * jnp.arange(basis_count).astype(jnp.float32)
    radial_basis = jnp.exp(-jnp.square((squared[None, :] - centers_sq[:, None]) / spacing))
    latent_in = (
        center_proj + partner_proj + jnp.dot(radial_weight.T, radial_basis, precision=highest)
    )
    first_hidden = jax.nn.silu(latent_in)
    second = first_hidden + jax.nn.silu(jnp.dot(mix_weight.T, first_hidden, precision=highest))
    vector_gain = jnp.dot(channel_weight[0].T, second, precision=highest)
    tensor_gain = jnp.dot(channel_weight[1].T, second, precision=highest)
    bond_vector = displace / cutoff_radius
    along_partner = jnp.sum(bond_vector[:, None, :] * partner_vecs, axis=0)
    along_center = jnp.sum(bond_vector[:, None, :] * center_vecs, axis=0)
    inner_product = jnp.sum(center_vecs * partner_vecs, axis=0)
    scaled_sq = squared / (cutoff_radius * cutoff_radius)
    quadratic = along_center * along_partner - scaled_sq[None, :] * inner_product / 3.0
    mixed_latent = second + vector_gain * along_partner + tensor_gain * quadratic
    readout = jnp.dot(
        out_weight,
        jax.nn.silu(jnp.dot(read_weight.T, mixed_latent, precision=highest)),
        precision=highest,
    )
    envelope = 1.0 / (1.0 + scaled_sq)
    return envelope * readout


def shift(payload, direction, distance):
    return from_behind(payload, ("gx", "gy", "gz")[direction], distance)


def halving_steps():
    steps = []
    for axis in ("gx", "gz", "gy"):
        size = lax.axis_size(axis)
        distance = 1
        while distance < size:
            steps.append((axis, distance, size))
            distance *= 2
    return steps


def sum_over_devices(rows):
    steps = halving_steps()
    if any(size & (size - 1) for _, _, size in steps):
        return lax.psum(rows, ("gx", "gy", "gz"))
    halvings = min(halving_count, len(steps))
    padded = jnp.pad(rows, ((0, (-rows.shape[0]) % (2**halvings)), (0, 0)))
    for axis, distance, size in steps[:halvings]:
        upper = (lax.axis_index(axis) // distance) % 2 == 1
        half = padded.shape[0] // 2
        low, high = padded[:half], padded[half:]
        keep = jnp.where(upper, high, low)
        send = jnp.where(upper, low, high)
        padded = keep + lax.ppermute(send, axis, [(i, i ^ distance) for i in range(size)])
    for axis, distance, size in steps[halvings:]:
        padded = padded + lax.ppermute(padded, axis, [(i, i ^ distance) for i in range(size)])
    for axis, distance, size in reversed(steps[:halvings]):
        upper = (lax.axis_index(axis) // distance) % 2 == 1
        other = lax.ppermute(padded, axis, [(i, i ^ distance) for i in range(size)])
        padded = jnp.where(
            upper, jnp.concatenate([other, padded]), jnp.concatenate([padded, other])
        )
    return padded[: rows.shape[0]]


def one_hot(rows, slots):
    return (jnp.arange(slots, dtype=jnp.int32)[:, None] == rows[None, :]).astype(jnp.float32)


def per_device(
    scalars,
    vectors,
    positions,
    species,
    atom_count,
    energy_weight,
    local_pairs,
    face_pairs,
    tile_counts,
    w_center,
    w_partner,
    w_radial,
    species_embed,
    w_mix,
    w_channel,
    w_read,
    w_out,
    species_energy,
):
    scalar_in = scalars[0, 0, 0]
    vector_in = vectors[0, 0, 0]
    coords = positions[0, 0, 0]
    weights_here = energy_weight[0, 0, 0]
    live_counts = tile_counts[0, 0, 0]
    local_list = local_pairs[0, 0, 0]
    face_list = face_pairs[0, 0, 0]
    channels, atom_slots = scalar_in.shape
    vector_rows = 3 * channels
    table_rows = channels + vector_rows + 3
    kind_count = species_energy.shape[0]
    local_slots = local_list.shape[1]
    face_slots = face_list.shape[2]
    species_hot = (
        species[0, 0, 0][None, :] == jnp.arange(kind_count, dtype=jnp.int32)[:, None]
    ).astype(jnp.float32)
    valid_atoms = (jnp.arange(atom_slots, dtype=jnp.int32) < atom_count[0, 0, 0]).astype(
        jnp.float32
    )

    edge_params = (w_radial, w_mix, w_channel, w_read, w_out)
    vector_flat = vector_in.reshape(vector_rows, atom_slots)
    own_table = jnp.concatenate([scalar_in, vector_flat, coords], axis=0)
    species_row = species[0, 0, 0].astype(jnp.float32)
    packet = jnp.concatenate([own_table, weights_here[None, :], species_row[None, :]], axis=0)
    arrived = [shift(packet, direction, -1) for direction in range(3)]
    far_tables = [incoming[:table_rows] for incoming in arrived]
    partner_weights = [weights_here] + [incoming[table_rows] for incoming in arrived]
    partner_species = [species_hot] + [
        (incoming[table_rows + 1][None, :] == jnp.arange(kind_count, dtype=jnp.float32)[:, None]).astype(
            jnp.float32
        )
        for incoming in arrived
    ]

    center_rows = jnp.concatenate([local_list[0]] + [face_list[d, 0] for d in range(3)])
    partner_rows = [local_list[1]] + [face_list[d, 1] for d in range(3)]
    center_hot = one_hot(center_rows, atom_slots)
    partner_hot = [one_hot(rows, atom_slots) for rows in partner_rows]
    slot_sizes = [local_slots] + [face_slots] * 3
    live_mask = jnp.concatenate(
        [
            (jnp.arange(size, dtype=jnp.int32) < live_counts[tile]).astype(jnp.float32)
            for tile, size in enumerate(slot_sizes)
        ]
    )
    offset = jnp.concatenate(
        [jnp.zeros((3, local_slots), jnp.float32)]
        + [
            jnp.broadcast_to(
                cell_edge * (jnp.arange(3) == d).astype(jnp.float32)[:, None], (3, face_slots)
            )
            for d in range(3)
        ],
        axis=1,
    )
    pair_weight = jnp.dot(weights_here, center_hot, precision=highest) + jnp.concatenate(
        [
            jnp.dot(weight_row, hot, precision=highest)
            for weight_row, hot in zip(partner_weights, partner_hot)
        ]
    )

    def pair_loss(center_matrix, partner_matrix, embed_table, params_in, own_in, far_in):
        def projected(matrix, embed_row, table, hot_kinds):
            proj = jnp.dot(matrix.T, table[:channels], precision=highest) + jnp.dot(
                embed_row.T, hot_kinds, precision=highest
            )
            return jnp.concatenate([proj, table[channels:]], axis=0)

        center_in = projected(center_matrix, embed_table[0], own_in, species_hot)
        partner_in = [
            projected(partner_matrix, embed_table[1], table, hot_kinds)
            for table, hot_kinds in zip([own_in] + list(far_in), partner_species)
        ]
        center_side = jnp.dot(center_in, center_hot, precision=highest)
        partner_side = jnp.concatenate(
            [jnp.dot(table, hot, precision=highest) for table, hot in zip(partner_in, partner_hot)],
            axis=1,
        )
        pair_count = center_side.shape[1]
        displace = (
            partner_side[channels + vector_rows :] + offset - center_side[channels + vector_rows :]
        )
        energies = edge_energy(
            params_in,
            center_side[:channels],
            partner_side[:channels],
            center_side[channels : channels + vector_rows].reshape(3, channels, pair_count),
            partner_side[channels : channels + vector_rows].reshape(3, channels, pair_count),
            displace,
        )
        halves = 0.5 * live_mask * energies
        return jnp.sum(halves * pair_weight), halves

    weighted_sum, pull_back, halves = jax.vjp(
        pair_loss, w_center, w_partner, species_embed, edge_params, own_table, far_tables,
        has_aux=True,
    )
    center_matrix_grad, partner_matrix_grad, embed_grad, param_grad, own_grad, far_grad = pull_back(
        jnp.ones_like(weighted_sum)
    )
    center_energy = jnp.dot(center_hot, halves, precision=highest)
    starts = [0, local_slots] + [local_slots + face_slots * (d + 1) for d in range(3)]
    partner_energy = [
        jnp.dot(hot, halves[starts[tile] : starts[tile + 1]], precision=highest)
        for tile, hot in enumerate(partner_hot)
    ]

    returned = [
        shift(jnp.concatenate([far_grad[d], partner_energy[d + 1][None, :]], axis=0), d, 1)
        for d in range(3)
    ]
    table_grad = own_grad
    for back_in in returned:
        table_grad = table_grad + back_in[:table_rows]
    pair_energy = center_energy + partner_energy[0]
    for back_in in returned:
        pair_energy = pair_energy + back_in[table_rows]
    scalar_grad = table_grad[:channels]
    vector_grad = table_grad[channels : channels + vector_rows].reshape(3, channels, atom_slots)
    coord_grad = table_grad[channels + vector_rows :]

    self_energy = valid_atoms * jnp.dot(species_energy, species_hot, precision=highest)
    reference_grad = jnp.dot(species_hot, weights_here * valid_atoms, precision=highest)
    lanes = channels

    def as_rows(piece):
        flat = piece.reshape(-1)
        return jnp.pad(flat, (0, (-flat.shape[0]) % lanes)).reshape(-1, lanes)

    grad_pieces = [
        center_matrix_grad,
        partner_matrix_grad,
        param_grad[0],
        embed_grad,
        param_grad[1],
        param_grad[2],
        param_grad[3],
    ]
    tail = jnp.concatenate([param_grad[4].reshape(-1), reference_grad])
    sizes = [piece.size for piece in grad_pieces] + [tail.shape[0]]
    local_rows = jnp.concatenate([as_rows(piece) for piece in grad_pieces] + [as_rows(tail)], axis=0)
    domain_total = lax.axis_size("gx") * lax.axis_size("gy") * lax.axis_size("gz")
    summed = sum_over_devices(local_rows) / domain_total
    weight_grad = summed.reshape(-1)[: sum(sizes)]
    atom_energy = self_energy + pair_energy
    return (
        atom_energy[None, None, None],
        coord_grad[None, None, None],
        scalar_grad[None, None, None],
        vector_grad[None, None, None],
        weight_grad,
    )


def solution(mesh):
    return jax.shard_map(
        per_device,
        mesh=mesh,
        in_specs=(
            P("gx", "gy", "gz", None, None),
            P("gx", "gy", "gz", None, None, None),
            P("gx", "gy", "gz", None, None),
            P("gx", "gy", "gz", None),
            P("gx", "gy", "gz"),
            P("gx", "gy", "gz", None),
            P("gx", "gy", "gz", None, None),
            P("gx", "gy", "gz", None, None, None),
            P("gx", "gy", "gz", None),
            P(),
            P(),
            P(),
            P(),
            P(),
            P(),
            P(),
            P(),
            P(),
        ),
        out_specs=(
            P("gx", "gy", "gz", None),
            P("gx", "gy", "gz", None, None),
            P("gx", "gy", "gz", None, None),
            P("gx", "gy", "gz", None, None, None),
            P(),
        ),
        check_vma=False,
    )
```

```python
import jax
import jax.numpy as jnp
from jax import lax
from jax.sharding import PartitionSpec as P

cutoff_radius = 5.0
cell_edge = 6.0
highest = lax.Precision.HIGHEST
halving_count = 3


def from_behind(block, axis, distance):
    devices = range(lax.axis_size(axis))
    route = [((i - distance) % len(devices), i) for i in devices]
    return lax.ppermute(block, axis, route)


def edge_energy(edge_params, center_proj, partner_proj, center_vecs, partner_vecs, displace):
    radial_weight, mix_weight, channel_weight, read_weight, out_weight = edge_params
    squared = jnp.sum(displace * displace, axis=0)
    basis_count = radial_weight.shape[0]
    spacing = cutoff_radius * cutoff_radius / (basis_count - 1)
    centers_sq = spacing * jnp.arange(basis_count).astype(jnp.float32)
    radial_basis = jnp.exp(-jnp.square((squared[None, :] - centers_sq[:, None]) / spacing))
    latent_in = (
        center_proj + partner_proj + jnp.dot(radial_weight.T, radial_basis, precision=highest)
    )
    first_hidden = jax.nn.silu(latent_in)
    second = first_hidden + jax.nn.silu(jnp.dot(mix_weight.T, first_hidden, precision=highest))
    vector_gain = jnp.dot(channel_weight[0].T, second, precision=highest)
    tensor_gain = jnp.dot(channel_weight[1].T, second, precision=highest)
    bond_vector = displace / cutoff_radius
    along_partner = jnp.sum(bond_vector[:, None, :] * partner_vecs, axis=0)
    along_center = jnp.sum(bond_vector[:, None, :] * center_vecs, axis=0)
    inner_product = jnp.sum(center_vecs * partner_vecs, axis=0)
    scaled_sq = squared / (cutoff_radius * cutoff_radius)
    quadratic = along_center * along_partner - scaled_sq[None, :] * inner_product / 3.0
    mixed_latent = second + vector_gain * along_partner + tensor_gain * quadratic
    readout = jnp.dot(
        out_weight,
        jax.nn.silu(jnp.dot(read_weight.T, mixed_latent, precision=highest)),
        precision=highest,
    )
    envelope = 1.0 / (1.0 + scaled_sq)
    return envelope * readout


def shift(payload, direction, distance):
    return from_behind(payload, ("gx", "gy", "gz")[direction], distance)


def halving_steps():
    steps = []
    for axis in ("gx", "gz", "gy"):
        size = lax.axis_size(axis)
        distance = 1
        while distance < size:
            steps.append((axis, distance, size))
            distance *= 2
    return steps


def sum_over_devices(rows):
    steps = halving_steps()
    if any(size & (size - 1) for _, _, size in steps):
        return lax.psum(rows, ("gx", "gy", "gz"))
    halvings = min(halving_count, len(steps))
    padded = jnp.pad(rows, ((0, (-rows.shape[0]) % (2**halvings)), (0, 0)))
    for axis, distance, size in steps[:halvings]:
        upper = (lax.axis_index(axis) // distance) % 2 == 1
        half = padded.shape[0] // 2
        low, high = padded[:half], padded[half:]
        keep = jnp.where(upper, high, low)
        send = jnp.where(upper, low, high)
        padded = keep + lax.ppermute(send, axis, [(i, i ^ distance) for i in range(size)])
    for axis, distance, size in steps[halvings:]:
        padded = padded + lax.ppermute(padded, axis, [(i, i ^ distance) for i in range(size)])
    for axis, distance, size in reversed(steps[:halvings]):
        upper = (lax.axis_index(axis) // distance) % 2 == 1
        other = lax.ppermute(padded, axis, [(i, i ^ distance) for i in range(size)])
        padded = jnp.where(
            upper, jnp.concatenate([other, padded]), jnp.concatenate([padded, other])
        )
    return padded[: rows.shape[0]]


def one_hot(rows, slots):
    return (jnp.arange(slots, dtype=jnp.int32)[:, None] == rows[None, :]).astype(jnp.float32)


def per_device(
    scalars,
    vectors,
    positions,
    species,
    atom_count,
    energy_weight,
    local_pairs,
    face_pairs,
    tile_counts,
    w_center,
    w_partner,
    w_radial,
    species_embed,
    w_mix,
    w_channel,
    w_read,
    w_out,
    species_energy,
):
    scalar_in = scalars[0, 0, 0]
    vector_in = vectors[0, 0, 0]
    coords = positions[0, 0, 0]
    weights_here = energy_weight[0, 0, 0]
    live_counts = tile_counts[0, 0, 0]
    local_list = local_pairs[0, 0, 0]
    face_list = face_pairs[0, 0, 0]
    channels, atom_slots = scalar_in.shape
    vector_rows = 3 * channels
    table_rows = channels + vector_rows + 3
    kind_count = species_energy.shape[0]
    local_slots = local_list.shape[1]
    face_slots = face_list.shape[2]
    species_hot = (
        species[0, 0, 0][None, :] == jnp.arange(kind_count, dtype=jnp.int32)[:, None]
    ).astype(jnp.float32)
    valid_atoms = (jnp.arange(atom_slots, dtype=jnp.int32) < atom_count[0, 0, 0]).astype(
        jnp.float32
    )

    edge_params = (w_radial, w_mix, w_channel, w_read, w_out)
    vector_flat = vector_in.reshape(vector_rows, atom_slots)
    own_table = jnp.concatenate([scalar_in, vector_flat, coords], axis=0)
    species_row = species[0, 0, 0].astype(jnp.float32)
    packet = jnp.concatenate([own_table, weights_here[None, :], species_row[None, :]], axis=0)
    arrived = [shift(packet, direction, -1) for direction in range(3)]
    far_tables = [incoming[:table_rows] for incoming in arrived]
    partner_weights = [weights_here] + [incoming[table_rows] for incoming in arrived]
    partner_species = [species_hot] + [
        (incoming[table_rows + 1][None, :] == jnp.arange(kind_count, dtype=jnp.float32)[:, None]).astype(
            jnp.float32
        )
        for incoming in arrived
    ]

    center_rows = jnp.concatenate([local_list[0]] + [face_list[d, 0] for d in range(3)])
    partner_rows = [local_list[1]] + [face_list[d, 1] for d in range(3)]
    center_hot = one_hot(center_rows, atom_slots)
    partner_hot = [one_hot(rows, atom_slots) for rows in partner_rows]
    slot_sizes = [local_slots] + [face_slots] * 3
    live_mask = jnp.concatenate(
        [
            (jnp.arange(size, dtype=jnp.int32) < live_counts[tile]).astype(jnp.float32)
            for tile, size in enumerate(slot_sizes)
        ]
    )
    offset = jnp.concatenate(
        [jnp.zeros((3, local_slots), jnp.float32)]
        + [
            jnp.broadcast_to(
                cell_edge * (jnp.arange(3) == d).astype(jnp.float32)[:, None], (3, face_slots)
            )
            for d in range(3)
        ],
        axis=1,
    )
    local_center_hot = center_hot[:, :local_slots]
    face_center_hot = center_hot[:, local_slots:]
    local_weight = jnp.dot(weights_here, local_center_hot, precision=highest) + jnp.dot(
        weights_here, partner_hot[0], precision=highest
    )
    face_weight = jnp.dot(weights_here, face_center_hot, precision=highest) + jnp.concatenate(
        [
            jnp.dot(weight_row, hot, precision=highest)
            for weight_row, hot in zip(partner_weights[1:], partner_hot[1:])
        ]
    )

    def tile_halves(params_in, center_side, partner_side, mask, shift_by):
        pair_count = center_side.shape[1]
        partner_coords = partner_side[channels + vector_rows :]
        if shift_by is not None:
            partner_coords = partner_coords + shift_by
        displace = partner_coords - center_side[channels + vector_rows :]
        energies = edge_energy(
            params_in,
            center_side[:channels],
            partner_side[:channels],
            center_side[channels : channels + vector_rows].reshape(3, channels, pair_count),
            partner_side[channels : channels + vector_rows].reshape(3, channels, pair_count),
            displace,
        )
        return 0.5 * mask * energies

    def pair_loss(center_matrix, partner_matrix, embed_table, params_in, own_in, far_in):
        def projected(matrix, embed_row, table, hot_kinds):
            proj = jnp.dot(matrix.T, table[:channels], precision=highest) + jnp.dot(
                embed_row.T, hot_kinds, precision=highest
            )
            return jnp.concatenate([proj, table[channels:]], axis=0)

        center_in = projected(center_matrix, embed_table[0], own_in, species_hot)
        partner_in = [
            projected(partner_matrix, embed_table[1], table, hot_kinds)
            for table, hot_kinds in zip([own_in] + list(far_in), partner_species)
        ]
        local_halves = tile_halves(
            params_in,
            jnp.dot(center_in, local_center_hot, precision=highest),
            jnp.dot(partner_in[0], partner_hot[0], precision=highest),
            live_mask[:local_slots],
            None,
        )
        face_halves = tile_halves(
            params_in,
            jnp.dot(center_in, face_center_hot, precision=highest),
            jnp.concatenate(
                [
                    jnp.dot(table, hot, precision=highest)
                    for table, hot in zip(partner_in[1:], partner_hot[1:])
                ],
                axis=1,
            ),
            live_mask[local_slots:],
            offset[:, local_slots:],
        )
        total = jnp.sum(local_halves * local_weight) + jnp.sum(face_halves * face_weight)
        return total, jnp.concatenate([local_halves, face_halves])

    weighted_sum, pull_back, halves = jax.vjp(
        pair_loss, w_center, w_partner, species_embed, edge_params, own_table, far_tables,
        has_aux=True,
    )
    center_matrix_grad, partner_matrix_grad, embed_grad, param_grad, own_grad, far_grad = pull_back(
        jnp.ones_like(weighted_sum)
    )
    center_energy = jnp.dot(center_hot, halves, precision=highest)
    starts = [0, local_slots] + [local_slots + face_slots * (d + 1) for d in range(3)]
    partner_energy = [
        jnp.dot(hot, halves[starts[tile] : starts[tile + 1]], precision=highest)
        for tile, hot in enumerate(partner_hot)
    ]

    returned = [
        shift(jnp.concatenate([far_grad[d], partner_energy[d + 1][None, :]], axis=0), d, 1)
        for d in range(3)
    ]
    table_grad = own_grad
    for back_in in returned:
        table_grad = table_grad + back_in[:table_rows]
    pair_energy = center_energy + partner_energy[0]
    for back_in in returned:
        pair_energy = pair_energy + back_in[table_rows]
    scalar_grad = table_grad[:channels]
    vector_grad = table_grad[channels : channels + vector_rows].reshape(3, channels, atom_slots)
    coord_grad = table_grad[channels + vector_rows :]

    self_energy = valid_atoms * jnp.dot(species_energy, species_hot, precision=highest)
    reference_grad = jnp.dot(species_hot, weights_here * valid_atoms, precision=highest)
    lanes = channels

    def as_rows(piece):
        flat = piece.reshape(-1)
        return jnp.pad(flat, (0, (-flat.shape[0]) % lanes)).reshape(-1, lanes)

    grad_pieces = [
        center_matrix_grad,
        partner_matrix_grad,
        param_grad[0],
        embed_grad,
        param_grad[1],
        param_grad[2],
        param_grad[3],
    ]
    tail = jnp.concatenate([param_grad[4].reshape(-1), reference_grad])
    sizes = [piece.size for piece in grad_pieces] + [tail.shape[0]]
    local_rows = jnp.concatenate([as_rows(piece) for piece in grad_pieces] + [as_rows(tail)], axis=0)
    domain_total = lax.axis_size("gx") * lax.axis_size("gy") * lax.axis_size("gz")
    summed = sum_over_devices(local_rows) / domain_total
    weight_grad = summed.reshape(-1)[: sum(sizes)]
    atom_energy = self_energy + pair_energy
    return (
        atom_energy[None, None, None],
        coord_grad[None, None, None],
        scalar_grad[None, None, None],
        vector_grad[None, None, None],
        weight_grad,
    )


def solution(mesh):
    return jax.shard_map(
        per_device,
        mesh=mesh,
        in_specs=(
            P("gx", "gy", "gz", None, None),
            P("gx", "gy", "gz", None, None, None),
            P("gx", "gy", "gz", None, None),
            P("gx", "gy", "gz", None),
            P("gx", "gy", "gz"),
            P("gx", "gy", "gz", None),
            P("gx", "gy", "gz", None, None),
            P("gx", "gy", "gz", None, None, None),
            P("gx", "gy", "gz", None),
            P(),
            P(),
            P(),
            P(),
            P(),
            P(),
            P(),
            P(),
            P(),
        ),
        out_specs=(
            P("gx", "gy", "gz", None),
            P("gx", "gy", "gz", None, None),
            P("gx", "gy", "gz", None, None),
            P("gx", "gy", "gz", None, None, None),
            P(),
        ),
        check_vma=False,
    )
```

```python
import jax
import jax.numpy as jnp
from jax import lax
from jax.sharding import PartitionSpec as P

cutoff_radius = 5.0
cell_edge = 6.0
highest = lax.Precision.HIGHEST
halving_count = 3


def from_behind(block, axis, distance):
    devices = range(lax.axis_size(axis))
    route = [((i - distance) % len(devices), i) for i in devices]
    return lax.ppermute(block, axis, route)


def edge_energy(edge_params, center_proj, partner_proj, center_vecs, partner_vecs, displace):
    radial_weight, mix_weight, channel_weight, read_weight, out_weight = edge_params
    squared = jnp.sum(displace * displace, axis=0)
    basis_count = radial_weight.shape[0]
    spacing = cutoff_radius * cutoff_radius / (basis_count - 1)
    centers_sq = spacing * jnp.arange(basis_count).astype(jnp.float32)
    radial_basis = jnp.exp(-jnp.square((squared[None, :] - centers_sq[:, None]) / spacing))
    latent_in = (
        center_proj + partner_proj + jnp.dot(radial_weight.T, radial_basis, precision=lax.Precision.HIGH)
    )
    first_hidden = jax.nn.silu(latent_in)
    second = first_hidden + jax.nn.silu(jnp.dot(mix_weight.T, first_hidden, precision=lax.Precision.HIGH))
    vector_gain = jnp.dot(channel_weight[0].T, second, precision=lax.Precision.HIGH)
    tensor_gain = jnp.dot(channel_weight[1].T, second, precision=lax.Precision.HIGH)
    bond_vector = displace / cutoff_radius
    along_partner = jnp.sum(bond_vector[:, None, :] * partner_vecs, axis=0)
    along_center = jnp.sum(bond_vector[:, None, :] * center_vecs, axis=0)
    inner_product = jnp.sum(center_vecs * partner_vecs, axis=0)
    scaled_sq = squared / (cutoff_radius * cutoff_radius)
    quadratic = along_center * along_partner - scaled_sq[None, :] * inner_product / 3.0
    mixed_latent = second + vector_gain * along_partner + tensor_gain * quadratic
    readout = jnp.dot(
        out_weight,
        jax.nn.silu(jnp.dot(read_weight.T, mixed_latent, precision=lax.Precision.HIGH)),
        precision=highest,
    )
    envelope = 1.0 / (1.0 + scaled_sq)
    return envelope * readout


def shift(payload, direction, distance):
    return from_behind(payload, ("gx", "gy", "gz")[direction], distance)


def halving_steps():
    steps = []
    for axis in ("gx", "gz", "gy"):
        size = lax.axis_size(axis)
        distance = 1
        while distance < size:
            steps.append((axis, distance, size))
            distance *= 2
    return steps


def sum_over_devices(rows):
    steps = halving_steps()
    if any(size & (size - 1) for _, _, size in steps):
        return lax.psum(rows, ("gx", "gy", "gz"))
    halvings = min(halving_count, len(steps))
    padded = jnp.pad(rows, ((0, (-rows.shape[0]) % (2**halvings)), (0, 0)))
    for axis, distance, size in steps[:halvings]:
        upper = (lax.axis_index(axis) // distance) % 2 == 1
        half = padded.shape[0] // 2
        low, high = padded[:half], padded[half:]
        keep = jnp.where(upper, high, low)
        send = jnp.where(upper, low, high)
        padded = keep + lax.ppermute(send, axis, [(i, i ^ distance) for i in range(size)])
    for axis, distance, size in steps[halvings:]:
        padded = padded + lax.ppermute(padded, axis, [(i, i ^ distance) for i in range(size)])
    for axis, distance, size in reversed(steps[:halvings]):
        upper = (lax.axis_index(axis) // distance) % 2 == 1
        other = lax.ppermute(padded, axis, [(i, i ^ distance) for i in range(size)])
        padded = jnp.where(
            upper, jnp.concatenate([other, padded]), jnp.concatenate([padded, other])
        )
    return padded[: rows.shape[0]]


def one_hot(rows, slots):
    return (jnp.arange(slots, dtype=jnp.int32)[:, None] == rows[None, :]).astype(jnp.float32)


def per_device(
    scalars,
    vectors,
    positions,
    species,
    atom_count,
    energy_weight,
    local_pairs,
    face_pairs,
    tile_counts,
    w_center,
    w_partner,
    w_radial,
    species_embed,
    w_mix,
    w_channel,
    w_read,
    w_out,
    species_energy,
):
    scalar_in = scalars[0, 0, 0]
    vector_in = vectors[0, 0, 0]
    coords = positions[0, 0, 0]
    weights_here = energy_weight[0, 0, 0]
    live_counts = tile_counts[0, 0, 0]
    local_list = local_pairs[0, 0, 0]
    face_list = face_pairs[0, 0, 0]
    channels, atom_slots = scalar_in.shape
    vector_rows = 3 * channels
    table_rows = channels + vector_rows + 3
    kind_count = species_energy.shape[0]
    local_slots = local_list.shape[1]
    face_slots = face_list.shape[2]
    species_hot = (
        species[0, 0, 0][None, :] == jnp.arange(kind_count, dtype=jnp.int32)[:, None]
    ).astype(jnp.float32)
    valid_atoms = (jnp.arange(atom_slots, dtype=jnp.int32) < atom_count[0, 0, 0]).astype(
        jnp.float32
    )

    edge_params = (w_radial, w_mix, w_channel, w_read, w_out)
    vector_flat = vector_in.reshape(vector_rows, atom_slots)
    own_table = jnp.concatenate([scalar_in, vector_flat, coords], axis=0)
    species_row = species[0, 0, 0].astype(jnp.float32)
    packet = jnp.concatenate([own_table, weights_here[None, :], species_row[None, :]], axis=0)
    arrived = [shift(packet, direction, -1) for direction in range(3)]
    far_tables = [incoming[:table_rows] for incoming in arrived]
    partner_weights = [weights_here] + [incoming[table_rows] for incoming in arrived]
    partner_species = [species_hot] + [
        (incoming[table_rows + 1][None, :] == jnp.arange(kind_count, dtype=jnp.float32)[:, None]).astype(
            jnp.float32
        )
        for incoming in arrived
    ]

    center_rows = jnp.concatenate([local_list[0]] + [face_list[d, 0] for d in range(3)])
    partner_rows = [local_list[1]] + [face_list[d, 1] for d in range(3)]
    center_hot = one_hot(center_rows, atom_slots)
    partner_hot = [one_hot(rows, atom_slots) for rows in partner_rows]
    slot_sizes = [local_slots] + [face_slots] * 3
    live_mask = jnp.concatenate(
        [
            (jnp.arange(size, dtype=jnp.int32) < live_counts[tile]).astype(jnp.float32)
            for tile, size in enumerate(slot_sizes)
        ]
    )
    offset = jnp.concatenate(
        [jnp.zeros((3, local_slots), jnp.float32)]
        + [
            jnp.broadcast_to(
                cell_edge * (jnp.arange(3) == d).astype(jnp.float32)[:, None], (3, face_slots)
            )
            for d in range(3)
        ],
        axis=1,
    )
    pair_weight = jnp.dot(weights_here, center_hot, precision=lax.Precision.HIGH) + jnp.concatenate(
        [
            jnp.dot(weight_row, hot, precision=lax.Precision.HIGH)
            for weight_row, hot in zip(partner_weights, partner_hot)
        ]
    )

    def pair_loss(center_matrix, partner_matrix, embed_table, params_in, own_in, far_in):
        def projected(matrix, embed_row, table, hot_kinds):
            proj = jnp.dot(matrix.T, table[:channels], precision=lax.Precision.HIGH) + jnp.dot(
                embed_row.T, hot_kinds, precision=highest
            )
            return jnp.concatenate([proj, table[channels:]], axis=0)

        center_in = projected(center_matrix, embed_table[0], own_in, species_hot)
        partner_in = [
            projected(partner_matrix, embed_table[1], table, hot_kinds)
            for table, hot_kinds in zip([own_in] + list(far_in), partner_species)
        ]
        center_side = jnp.dot(center_in, center_hot, precision=lax.Precision.HIGH)
        partner_side = jnp.concatenate(
            [jnp.dot(table, hot, precision=lax.Precision.HIGH) for table, hot in zip(partner_in, partner_hot)],
            axis=1,
        )
        pair_count = center_side.shape[1]
        displace = (
            partner_side[channels + vector_rows :] + offset - center_side[channels + vector_rows :]
        )
        energies = edge_energy(
            params_in,
            center_side[:channels],
            partner_side[:channels],
            center_side[channels : channels + vector_rows].reshape(3, channels, pair_count),
            partner_side[channels : channels + vector_rows].reshape(3, channels, pair_count),
            displace,
        )
        halves = 0.5 * live_mask * energies
        return jnp.sum(halves * pair_weight), halves

    weighted_sum, pull_back, halves = jax.vjp(
        pair_loss, w_center, w_partner, species_embed, edge_params, own_table, far_tables,
        has_aux=True,
    )
    center_matrix_grad, partner_matrix_grad, embed_grad, param_grad, own_grad, far_grad = pull_back(
        jnp.ones_like(weighted_sum)
    )
    center_energy = jnp.dot(center_hot, halves, precision=lax.Precision.HIGH)
    starts = [0, local_slots] + [local_slots + face_slots * (d + 1) for d in range(3)]
    partner_energy = [
        jnp.dot(hot, halves[starts[tile] : starts[tile + 1]], precision=lax.Precision.HIGH)
        for tile, hot in enumerate(partner_hot)
    ]

    returned = [
        shift(jnp.concatenate([far_grad[d], partner_energy[d + 1][None, :]], axis=0), d, 1)
        for d in range(3)
    ]
    table_grad = own_grad
    for back_in in returned:
        table_grad = table_grad + back_in[:table_rows]
    pair_energy = center_energy + partner_energy[0]
    for back_in in returned:
        pair_energy = pair_energy + back_in[table_rows]
    scalar_grad = table_grad[:channels]
    vector_grad = table_grad[channels : channels + vector_rows].reshape(3, channels, atom_slots)
    coord_grad = table_grad[channels + vector_rows :]

    self_energy = valid_atoms * jnp.dot(species_energy, species_hot, precision=lax.Precision.HIGH)
    reference_grad = jnp.dot(species_hot, weights_here * valid_atoms, precision=lax.Precision.HIGH)
    lanes = channels

    def as_rows(piece):
        flat = piece.reshape(-1)
        return jnp.pad(flat, (0, (-flat.shape[0]) % lanes)).reshape(-1, lanes)

    grad_pieces = [
        center_matrix_grad,
        partner_matrix_grad,
        param_grad[0],
        embed_grad,
        param_grad[1],
        param_grad[2],
        param_grad[3],
    ]
    tail = jnp.concatenate([param_grad[4].reshape(-1), reference_grad])
    sizes = [piece.size for piece in grad_pieces] + [tail.shape[0]]
    local_rows = jnp.concatenate([as_rows(piece) for piece in grad_pieces] + [as_rows(tail)], axis=0)
    domain_total = lax.axis_size("gx") * lax.axis_size("gy") * lax.axis_size("gz")
    summed = sum_over_devices(local_rows) / domain_total
    weight_grad = summed.reshape(-1)[: sum(sizes)]
    atom_energy = self_energy + pair_energy
    return (
        atom_energy[None, None, None],
        coord_grad[None, None, None],
        scalar_grad[None, None, None],
        vector_grad[None, None, None],
        weight_grad,
    )


def solution(mesh):
    return jax.shard_map(
        per_device,
        mesh=mesh,
        in_specs=(
            P("gx", "gy", "gz", None, None),
            P("gx", "gy", "gz", None, None, None),
            P("gx", "gy", "gz", None, None),
            P("gx", "gy", "gz", None),
            P("gx", "gy", "gz"),
            P("gx", "gy", "gz", None),
            P("gx", "gy", "gz", None, None),
            P("gx", "gy", "gz", None, None, None),
            P("gx", "gy", "gz", None),
            P(),
            P(),
            P(),
            P(),
            P(),
            P(),
            P(),
            P(),
            P(),
        ),
        out_specs=(
            P("gx", "gy", "gz", None),
            P("gx", "gy", "gz", None, None),
            P("gx", "gy", "gz", None, None),
            P("gx", "gy", "gz", None, None, None),
            P(),
        ),
        check_vma=False,
    )
```

```python
import jax
import jax.numpy as jnp
from jax import lax
from jax.sharding import PartitionSpec as P

cutoff_radius = 5.0
cell_edge = 6.0
highest = lax.Precision.HIGHEST
halving_count = 3


def from_behind(block, axis, distance):
    devices = range(lax.axis_size(axis))
    route = [((i - distance) % len(devices), i) for i in devices]
    return lax.ppermute(block, axis, route)


def edge_energy(edge_params, center_proj, partner_proj, center_vecs, partner_vecs, displace):
    radial_weight, mix_weight, channel_weight, read_weight, out_weight = edge_params
    squared = jnp.sum(displace * displace, axis=0)
    basis_count = radial_weight.shape[0]
    spacing = cutoff_radius * cutoff_radius / (basis_count - 1)
    centers_sq = spacing * jnp.arange(basis_count).astype(jnp.float32)
    radial_basis = jnp.exp(-jnp.square((squared[None, :] - centers_sq[:, None]) / spacing))
    latent_in = (
        center_proj + partner_proj + jnp.dot(radial_weight.T, radial_basis, precision=lax.Precision.HIGH)
    )
    first_hidden = jax.nn.silu(latent_in)
    second = first_hidden + jax.nn.silu(jnp.dot(mix_weight.T, first_hidden, precision=lax.Precision.HIGH))
    vector_gain = jnp.dot(channel_weight[0].T, second, precision=lax.Precision.HIGH)
    tensor_gain = jnp.dot(channel_weight[1].T, second, precision=lax.Precision.HIGH)
    bond_vector = displace / cutoff_radius
    along_partner = jnp.sum(bond_vector[:, None, :] * partner_vecs, axis=0)
    along_center = jnp.sum(bond_vector[:, None, :] * center_vecs, axis=0)
    inner_product = jnp.sum(center_vecs * partner_vecs, axis=0)
    scaled_sq = squared / (cutoff_radius * cutoff_radius)
    quadratic = along_center * along_partner - scaled_sq[None, :] * inner_product / 3.0
    mixed_latent = second + vector_gain * along_partner + tensor_gain * quadratic
    readout = jnp.dot(
        out_weight,
        jax.nn.silu(jnp.dot(read_weight.T, mixed_latent, precision=lax.Precision.HIGH)),
        precision=highest,
    )
    envelope = 1.0 / (1.0 + scaled_sq)
    return envelope * readout


def shift(payload, direction, distance):
    return from_behind(payload, ("gx", "gy", "gz")[direction], distance)


def halving_steps():
    steps = []
    for axis in ("gx", "gz", "gy"):
        size = lax.axis_size(axis)
        distance = 1
        while distance < size:
            steps.append((axis, distance, size))
            distance *= 2
    return steps


def sum_over_devices(rows):
    steps = halving_steps()
    if any(size & (size - 1) for _, _, size in steps):
        return lax.psum(rows, ("gx", "gy", "gz"))
    halvings = min(halving_count, len(steps))
    padded = jnp.pad(rows, ((0, (-rows.shape[0]) % (2**halvings)), (0, 0)))
    for axis, distance, size in steps[:halvings]:
        upper = (lax.axis_index(axis) // distance) % 2 == 1
        half = padded.shape[0] // 2
        low, high = padded[:half], padded[half:]
        keep = jnp.where(upper, high, low)
        send = jnp.where(upper, low, high)
        padded = keep + lax.ppermute(send, axis, [(i, i ^ distance) for i in range(size)])
    for axis, distance, size in steps[halvings:]:
        padded = padded + lax.ppermute(padded, axis, [(i, i ^ distance) for i in range(size)])
    for axis, distance, size in reversed(steps[:halvings]):
        upper = (lax.axis_index(axis) // distance) % 2 == 1
        other = lax.ppermute(padded, axis, [(i, i ^ distance) for i in range(size)])
        padded = jnp.where(
            upper, jnp.concatenate([other, padded]), jnp.concatenate([padded, other])
        )
    return padded[: rows.shape[0]]


def one_hot(rows, slots):
    return (jnp.arange(slots, dtype=jnp.int32)[:, None] == rows[None, :]).astype(jnp.float32)


def per_device(
    scalars,
    vectors,
    positions,
    species,
    atom_count,
    energy_weight,
    local_pairs,
    face_pairs,
    tile_counts,
    w_center,
    w_partner,
    w_radial,
    species_embed,
    w_mix,
    w_channel,
    w_read,
    w_out,
    species_energy,
):
    scalar_in = scalars[0, 0, 0]
    vector_in = vectors[0, 0, 0]
    coords = positions[0, 0, 0]
    weights_here = energy_weight[0, 0, 0]
    live_counts = tile_counts[0, 0, 0]
    local_list = local_pairs[0, 0, 0]
    face_list = face_pairs[0, 0, 0]
    channels, atom_slots = scalar_in.shape
    vector_rows = 3 * channels
    table_rows = channels + vector_rows + 3
    kind_count = species_energy.shape[0]
    local_slots = local_list.shape[1]
    face_slots = face_list.shape[2]
    species_hot = (
        species[0, 0, 0][None, :] == jnp.arange(kind_count, dtype=jnp.int32)[:, None]
    ).astype(jnp.float32)
    valid_atoms = (jnp.arange(atom_slots, dtype=jnp.int32) < atom_count[0, 0, 0]).astype(
        jnp.float32
    )

    edge_params = (w_radial, w_mix, w_channel, w_read, w_out)
    vector_flat = vector_in.reshape(vector_rows, atom_slots)
    own_table = jnp.concatenate([scalar_in, vector_flat, coords], axis=0)
    species_row = species[0, 0, 0].astype(jnp.float32)
    packet = jnp.concatenate([own_table, weights_here[None, :], species_row[None, :]], axis=0)
    arrived = [shift(packet, direction, -1) for direction in range(3)]
    far_tables = [incoming[:table_rows] for incoming in arrived]
    partner_weights = [weights_here] + [incoming[table_rows] for incoming in arrived]
    partner_species = [species_hot] + [
        (incoming[table_rows + 1][None, :] == jnp.arange(kind_count, dtype=jnp.float32)[:, None]).astype(
            jnp.float32
        )
        for incoming in arrived
    ]

    center_rows = jnp.concatenate([local_list[0]] + [face_list[d, 0] for d in range(3)])
    partner_rows = [local_list[1]] + [face_list[d, 1] for d in range(3)]
    center_hot = one_hot(center_rows, atom_slots)
    partner_hot = [one_hot(rows, atom_slots) for rows in partner_rows]
    slot_sizes = [local_slots] + [face_slots] * 3
    live_mask = jnp.concatenate(
        [
            (jnp.arange(size, dtype=jnp.int32) < live_counts[tile]).astype(jnp.float32)
            for tile, size in enumerate(slot_sizes)
        ]
    )
    offset = jnp.concatenate(
        [jnp.zeros((3, local_slots), jnp.float32)]
        + [
            jnp.broadcast_to(
                cell_edge * (jnp.arange(3) == d).astype(jnp.float32)[:, None], (3, face_slots)
            )
            for d in range(3)
        ],
        axis=1,
    )
    pair_weight = jnp.dot(weights_here, center_hot, precision=lax.Precision.HIGH) + jnp.concatenate(
        [
            jnp.dot(weight_row, hot, precision=lax.Precision.HIGH)
            for weight_row, hot in zip(partner_weights, partner_hot)
        ]
    )

    def pair_loss(center_matrix, partner_matrix, embed_table, params_in, own_in, far_in):
        def projected(matrix, embed_row, table, hot_kinds):
            proj = jnp.dot(matrix.T, table[:channels], precision=lax.Precision.HIGH) + jnp.dot(
                embed_row.T, hot_kinds, precision=highest
            )
            return jnp.concatenate([proj, table[channels:]], axis=0)

        center_in = projected(center_matrix, embed_table[0], own_in, species_hot)
        partner_in = [
            projected(partner_matrix, embed_table[1], table, hot_kinds)
            for table, hot_kinds in zip([own_in] + list(far_in), partner_species)
        ]
        center_side = jnp.dot(center_in, center_hot, precision=highest)
        partner_side = jnp.concatenate(
            [jnp.dot(table, hot, precision=highest) for table, hot in zip(partner_in, partner_hot)],
            axis=1,
        )
        pair_count = center_side.shape[1]
        displace = (
            partner_side[channels + vector_rows :] + offset - center_side[channels + vector_rows :]
        )
        energies = edge_energy(
            params_in,
            center_side[:channels],
            partner_side[:channels],
            center_side[channels : channels + vector_rows].reshape(3, channels, pair_count),
            partner_side[channels : channels + vector_rows].reshape(3, channels, pair_count),
            displace,
        )
        halves = 0.5 * live_mask * energies
        return jnp.sum(halves * pair_weight), halves

    weighted_sum, pull_back, halves = jax.vjp(
        pair_loss, w_center, w_partner, species_embed, edge_params, own_table, far_tables,
        has_aux=True,
    )
    center_matrix_grad, partner_matrix_grad, embed_grad, param_grad, own_grad, far_grad = pull_back(
        jnp.ones_like(weighted_sum)
    )
    center_energy = jnp.dot(center_hot, halves, precision=lax.Precision.HIGH)
    starts = [0, local_slots] + [local_slots + face_slots * (d + 1) for d in range(3)]
    partner_energy = [
        jnp.dot(hot, halves[starts[tile] : starts[tile + 1]], precision=lax.Precision.HIGH)
        for tile, hot in enumerate(partner_hot)
    ]

    returned = [
        shift(jnp.concatenate([far_grad[d], partner_energy[d + 1][None, :]], axis=0), d, 1)
        for d in range(3)
    ]
    table_grad = own_grad
    for back_in in returned:
        table_grad = table_grad + back_in[:table_rows]
    pair_energy = center_energy + partner_energy[0]
    for back_in in returned:
        pair_energy = pair_energy + back_in[table_rows]
    scalar_grad = table_grad[:channels]
    vector_grad = table_grad[channels : channels + vector_rows].reshape(3, channels, atom_slots)
    coord_grad = table_grad[channels + vector_rows :]

    self_energy = valid_atoms * jnp.dot(species_energy, species_hot, precision=lax.Precision.HIGH)
    reference_grad = jnp.dot(species_hot, weights_here * valid_atoms, precision=lax.Precision.HIGH)
    lanes = channels

    def as_rows(piece):
        flat = piece.reshape(-1)
        return jnp.pad(flat, (0, (-flat.shape[0]) % lanes)).reshape(-1, lanes)

    grad_pieces = [
        center_matrix_grad,
        partner_matrix_grad,
        param_grad[0],
        embed_grad,
        param_grad[1],
        param_grad[2],
        param_grad[3],
    ]
    tail = jnp.concatenate([param_grad[4].reshape(-1), reference_grad])
    sizes = [piece.size for piece in grad_pieces] + [tail.shape[0]]
    local_rows = jnp.concatenate([as_rows(piece) for piece in grad_pieces] + [as_rows(tail)], axis=0)
    domain_total = lax.axis_size("gx") * lax.axis_size("gy") * lax.axis_size("gz")
    summed = sum_over_devices(local_rows) / domain_total
    weight_grad = summed.reshape(-1)[: sum(sizes)]
    atom_energy = self_energy + pair_energy
    return (
        atom_energy[None, None, None],
        coord_grad[None, None, None],
        scalar_grad[None, None, None],
        vector_grad[None, None, None],
        weight_grad,
    )


def solution(mesh):
    return jax.shard_map(
        per_device,
        mesh=mesh,
        in_specs=(
            P("gx", "gy", "gz", None, None),
            P("gx", "gy", "gz", None, None, None),
            P("gx", "gy", "gz", None, None),
            P("gx", "gy", "gz", None),
            P("gx", "gy", "gz"),
            P("gx", "gy", "gz", None),
            P("gx", "gy", "gz", None, None),
            P("gx", "gy", "gz", None, None, None),
            P("gx", "gy", "gz", None),
            P(),
            P(),
            P(),
            P(),
            P(),
            P(),
            P(),
            P(),
            P(),
        ),
        out_specs=(
            P("gx", "gy", "gz", None),
            P("gx", "gy", "gz", None, None),
            P("gx", "gy", "gz", None, None),
            P("gx", "gy", "gz", None, None, None),
            P(),
        ),
        check_vma=False,
    )
```

```python
import jax
import jax.numpy as jnp
from jax import lax
from jax.sharding import PartitionSpec as P

cutoff_radius = 5.0
cell_edge = 6.0
highest = lax.Precision.HIGHEST
halving_count = 3


def from_behind(block, axis, distance):
    devices = range(lax.axis_size(axis))
    route = [((i - distance) % len(devices), i) for i in devices]
    return lax.ppermute(block, axis, route)


def edge_energy(edge_params, center_proj, partner_proj, center_vecs, partner_vecs, displace):
    radial_weight, mix_weight, channel_weight, read_weight, out_weight = edge_params
    squared = jnp.sum(displace * displace, axis=0)
    basis_count = radial_weight.shape[0]
    spacing = cutoff_radius * cutoff_radius / (basis_count - 1)
    centers_sq = spacing * jnp.arange(basis_count).astype(jnp.float32)
    radial_basis = jnp.exp(-jnp.square((squared[None, :] - centers_sq[:, None]) / spacing))
    latent_in = (
        center_proj + partner_proj + jnp.dot(radial_weight.T, radial_basis, precision=lax.Precision.HIGH)
    )
    first_hidden = jax.nn.silu(latent_in)
    second = first_hidden + jax.nn.silu(jnp.dot(mix_weight.T, first_hidden, precision=lax.Precision.HIGH))
    vector_gain = jnp.dot(channel_weight[0].T, second, precision=lax.Precision.HIGH)
    tensor_gain = jnp.dot(channel_weight[1].T, second, precision=lax.Precision.HIGH)
    bond_vector = displace / cutoff_radius
    along_partner = jnp.sum(bond_vector[:, None, :] * partner_vecs, axis=0)
    along_center = jnp.sum(bond_vector[:, None, :] * center_vecs, axis=0)
    inner_product = jnp.sum(center_vecs * partner_vecs, axis=0)
    scaled_sq = squared / (cutoff_radius * cutoff_radius)
    quadratic = along_center * along_partner - scaled_sq[None, :] * inner_product / 3.0
    mixed_latent = second + vector_gain * along_partner + tensor_gain * quadratic
    readout = jnp.dot(
        out_weight,
        jax.nn.silu(jnp.dot(read_weight.T, mixed_latent, precision=lax.Precision.HIGH)),
        precision=highest,
    )
    envelope = 1.0 / (1.0 + scaled_sq)
    return envelope * readout


def shift(payload, direction, distance):
    return from_behind(payload, ("gx", "gy", "gz")[direction], distance)


def halving_steps():
    steps = []
    for axis in ("gx", "gz", "gy"):
        size = lax.axis_size(axis)
        distance = 1
        while distance < size:
            steps.append((axis, distance, size))
            distance *= 2
    return steps


def sum_over_devices(rows):
    steps = halving_steps()
    if any(size & (size - 1) for _, _, size in steps):
        return lax.psum(rows, ("gx", "gy", "gz"))
    halvings = min(halving_count, len(steps))
    padded = jnp.pad(rows, ((0, (-rows.shape[0]) % (2**halvings)), (0, 0)))
    for axis, distance, size in steps[:halvings]:
        upper = (lax.axis_index(axis) // distance) % 2 == 1
        half = padded.shape[0] // 2
        low, high = padded[:half], padded[half:]
        keep = jnp.where(upper, high, low)
        send = jnp.where(upper, low, high)
        padded = keep + lax.ppermute(send, axis, [(i, i ^ distance) for i in range(size)])
    for axis, distance, size in steps[halvings:]:
        padded = padded + lax.ppermute(padded, axis, [(i, i ^ distance) for i in range(size)])
    for axis, distance, size in reversed(steps[:halvings]):
        upper = (lax.axis_index(axis) // distance) % 2 == 1
        other = lax.ppermute(padded, axis, [(i, i ^ distance) for i in range(size)])
        padded = jnp.where(
            upper, jnp.concatenate([other, padded]), jnp.concatenate([padded, other])
        )
    return padded[: rows.shape[0]]


def one_hot(rows, slots):
    return (jnp.arange(slots, dtype=jnp.int32)[:, None] == rows[None, :]).astype(jnp.float32)


def per_device(
    scalars,
    vectors,
    positions,
    species,
    atom_count,
    energy_weight,
    local_pairs,
    face_pairs,
    tile_counts,
    w_center,
    w_partner,
    w_radial,
    species_embed,
    w_mix,
    w_channel,
    w_read,
    w_out,
    species_energy,
):
    scalar_in = scalars[0, 0, 0]
    vector_in = vectors[0, 0, 0]
    coords = positions[0, 0, 0]
    weights_here = energy_weight[0, 0, 0]
    live_counts = tile_counts[0, 0, 0]
    local_list = local_pairs[0, 0, 0]
    face_list = face_pairs[0, 0, 0]
    channels, atom_slots = scalar_in.shape
    vector_rows = 3 * channels
    table_rows = channels + vector_rows + 3
    kind_count = species_energy.shape[0]
    local_slots = local_list.shape[1]
    face_slots = face_list.shape[2]
    species_hot = (
        species[0, 0, 0][None, :] == jnp.arange(kind_count, dtype=jnp.int32)[:, None]
    ).astype(jnp.float32)
    valid_atoms = (jnp.arange(atom_slots, dtype=jnp.int32) < atom_count[0, 0, 0]).astype(
        jnp.float32
    )

    edge_params = (w_radial, w_mix, w_channel, w_read, w_out)
    vector_flat = vector_in.reshape(vector_rows, atom_slots)
    own_table = jnp.concatenate([scalar_in, vector_flat, coords], axis=0)
    species_row = species[0, 0, 0].astype(jnp.float32)
    packet = jnp.concatenate([own_table, weights_here[None, :], species_row[None, :]], axis=0)
    arrived = [shift(packet, direction, -1) for direction in range(3)]
    far_tables = [incoming[:table_rows] for incoming in arrived]
    partner_weights = [weights_here] + [incoming[table_rows] for incoming in arrived]
    partner_species = [species_hot] + [
        (incoming[table_rows + 1][None, :] == jnp.arange(kind_count, dtype=jnp.float32)[:, None]).astype(
            jnp.float32
        )
        for incoming in arrived
    ]

    center_rows = jnp.concatenate([local_list[0]] + [face_list[d, 0] for d in range(3)])
    partner_rows = [local_list[1]] + [face_list[d, 1] for d in range(3)]
    center_hot = one_hot(center_rows, atom_slots)
    partner_hot = [one_hot(rows, atom_slots) for rows in partner_rows]
    slot_sizes = [local_slots] + [face_slots] * 3
    live_mask = jnp.concatenate(
        [
            (jnp.arange(size, dtype=jnp.int32) < live_counts[tile]).astype(jnp.float32)
            for tile, size in enumerate(slot_sizes)
        ]
    )
    offset = jnp.concatenate(
        [jnp.zeros((3, local_slots), jnp.float32)]
        + [
            jnp.broadcast_to(
                cell_edge * (jnp.arange(3) == d).astype(jnp.float32)[:, None], (3, face_slots)
            )
            for d in range(3)
        ],
        axis=1,
    )
    pair_weight = jnp.dot(weights_here, center_hot, precision=lax.Precision.HIGH) + jnp.concatenate(
        [
            jnp.dot(weight_row, hot, precision=lax.Precision.HIGH)
            for weight_row, hot in zip(partner_weights, partner_hot)
        ]
    )

    def pair_loss(center_matrix, partner_matrix, embed_table, params_in, own_in, far_in):
        def projected(matrix, embed_row, table, hot_kinds):
            proj = jnp.dot(matrix.T, table[:channels], precision=lax.Precision.HIGH) + jnp.dot(
                embed_row.T, hot_kinds, precision=highest
            )
            return jnp.concatenate([proj, table[channels:]], axis=0)

        center_in = projected(center_matrix, embed_table[0], own_in, species_hot)
        partner_in = [
            projected(partner_matrix, embed_table[1], table, hot_kinds)
            for table, hot_kinds in zip([own_in] + list(far_in), partner_species)
        ]
        center_side = jnp.dot(center_in, center_hot, precision=lax.Precision.HIGH)
        partner_side = jnp.concatenate(
            [jnp.dot(table, hot, precision=lax.Precision.HIGH) for table, hot in zip(partner_in, partner_hot)],
            axis=1,
        )
        pair_count = center_side.shape[1]
        partner_coords = jnp.concatenate(
            [
                jnp.dot(table[channels + vector_rows :], hot, precision=highest)
                for table, hot in zip(partner_in, partner_hot)
            ],
            axis=1,
        )
        center_coords = jnp.dot(center_in[channels + vector_rows :], center_hot, precision=highest)
        displace = partner_coords + offset - center_coords
        energies = edge_energy(
            params_in,
            center_side[:channels],
            partner_side[:channels],
            center_side[channels : channels + vector_rows].reshape(3, channels, pair_count),
            partner_side[channels : channels + vector_rows].reshape(3, channels, pair_count),
            displace,
        )
        halves = 0.5 * live_mask * energies
        return jnp.sum(halves * pair_weight), halves

    weighted_sum, pull_back, halves = jax.vjp(
        pair_loss, w_center, w_partner, species_embed, edge_params, own_table, far_tables,
        has_aux=True,
    )
    center_matrix_grad, partner_matrix_grad, embed_grad, param_grad, own_grad, far_grad = pull_back(
        jnp.ones_like(weighted_sum)
    )
    center_energy = jnp.dot(center_hot, halves, precision=lax.Precision.HIGH)
    starts = [0, local_slots] + [local_slots + face_slots * (d + 1) for d in range(3)]
    partner_energy = [
        jnp.dot(hot, halves[starts[tile] : starts[tile + 1]], precision=lax.Precision.HIGH)
        for tile, hot in enumerate(partner_hot)
    ]

    returned = [
        shift(jnp.concatenate([far_grad[d], partner_energy[d + 1][None, :]], axis=0), d, 1)
        for d in range(3)
    ]
    table_grad = own_grad
    for back_in in returned:
        table_grad = table_grad + back_in[:table_rows]
    pair_energy = center_energy + partner_energy[0]
    for back_in in returned:
        pair_energy = pair_energy + back_in[table_rows]
    scalar_grad = table_grad[:channels]
    vector_grad = table_grad[channels : channels + vector_rows].reshape(3, channels, atom_slots)
    coord_grad = table_grad[channels + vector_rows :]

    self_energy = valid_atoms * jnp.dot(species_energy, species_hot, precision=lax.Precision.HIGH)
    reference_grad = jnp.dot(species_hot, weights_here * valid_atoms, precision=lax.Precision.HIGH)
    lanes = channels

    def as_rows(piece):
        flat = piece.reshape(-1)
        return jnp.pad(flat, (0, (-flat.shape[0]) % lanes)).reshape(-1, lanes)

    grad_pieces = [
        center_matrix_grad,
        partner_matrix_grad,
        param_grad[0],
        embed_grad,
        param_grad[1],
        param_grad[2],
        param_grad[3],
    ]
    tail = jnp.concatenate([param_grad[4].reshape(-1), reference_grad])
    sizes = [piece.size for piece in grad_pieces] + [tail.shape[0]]
    local_rows = jnp.concatenate([as_rows(piece) for piece in grad_pieces] + [as_rows(tail)], axis=0)
    domain_total = lax.axis_size("gx") * lax.axis_size("gy") * lax.axis_size("gz")
    summed = sum_over_devices(local_rows) / domain_total
    weight_grad = summed.reshape(-1)[: sum(sizes)]
    atom_energy = self_energy + pair_energy
    return (
        atom_energy[None, None, None],
        coord_grad[None, None, None],
        scalar_grad[None, None, None],
        vector_grad[None, None, None],
        weight_grad,
    )


def solution(mesh):
    return jax.shard_map(
        per_device,
        mesh=mesh,
        in_specs=(
            P("gx", "gy", "gz", None, None),
            P("gx", "gy", "gz", None, None, None),
            P("gx", "gy", "gz", None, None),
            P("gx", "gy", "gz", None),
            P("gx", "gy", "gz"),
            P("gx", "gy", "gz", None),
            P("gx", "gy", "gz", None, None),
            P("gx", "gy", "gz", None, None, None),
            P("gx", "gy", "gz", None),
            P(),
            P(),
            P(),
            P(),
            P(),
            P(),
            P(),
            P(),
            P(),
        ),
        out_specs=(
            P("gx", "gy", "gz", None),
            P("gx", "gy", "gz", None, None),
            P("gx", "gy", "gz", None, None),
            P("gx", "gy", "gz", None, None, None),
            P(),
        ),
        check_vma=False,
    )
```

```python
import jax
import jax.numpy as jnp
from jax import lax
from jax.sharding import PartitionSpec as P

cutoff_radius = 5.0
cell_edge = 6.0
highest = lax.Precision.HIGHEST
halving_count = 3


def from_behind(block, axis, distance):
    devices = range(lax.axis_size(axis))
    route = [((i - distance) % len(devices), i) for i in devices]
    return lax.ppermute(block, axis, route)


def edge_energy(edge_params, center_proj, partner_proj, center_vecs, partner_vecs, displace):
    radial_weight, mix_weight, channel_weight, read_weight, out_weight = edge_params
    squared = jnp.sum(displace * displace, axis=0)
    basis_count = radial_weight.shape[0]
    spacing = cutoff_radius * cutoff_radius / (basis_count - 1)
    centers_sq = spacing * jnp.arange(basis_count).astype(jnp.float32)
    radial_basis = jnp.exp(-jnp.square((squared[None, :] - centers_sq[:, None]) / spacing))
    latent_in = (
        center_proj + partner_proj + jnp.dot(radial_weight.T, radial_basis, precision=lax.Precision.HIGH)
    )
    first_hidden = jax.nn.silu(latent_in)
    second = first_hidden + jax.nn.silu(jnp.dot(mix_weight.T, first_hidden, precision=lax.Precision.HIGH))
    vector_gain = jnp.dot(channel_weight[0].T, second, precision=lax.Precision.HIGH)
    tensor_gain = jnp.dot(channel_weight[1].T, second, precision=lax.Precision.HIGH)
    bond_vector = displace / cutoff_radius
    along_partner = jnp.sum(bond_vector[:, None, :] * partner_vecs, axis=0)
    along_center = jnp.sum(bond_vector[:, None, :] * center_vecs, axis=0)
    inner_product = jnp.sum(center_vecs * partner_vecs, axis=0)
    scaled_sq = squared / (cutoff_radius * cutoff_radius)
    quadratic = along_center * along_partner - scaled_sq[None, :] * inner_product / 3.0
    mixed_latent = second + vector_gain * along_partner + tensor_gain * quadratic
    readout = jnp.dot(
        out_weight,
        jax.nn.silu(jnp.dot(read_weight.T, mixed_latent, precision=lax.Precision.HIGH)),
        precision=highest,
    )
    envelope = 1.0 / (1.0 + scaled_sq)
    return envelope * readout


def shift(payload, direction, distance):
    return from_behind(payload, ("gx", "gy", "gz")[direction], distance)


def halving_steps():
    steps = []
    for axis in ("gx", "gz", "gy"):
        size = lax.axis_size(axis)
        distance = 1
        while distance < size:
            steps.append((axis, distance, size))
            distance *= 2
    return steps


def exchange_partner(index, distance, size):
    if distance >= 2 and 2 * distance == size:
        unit = distance // 2
        digit, low = divmod(index, unit)
        return (3 - digit) * unit + low
    return index ^ distance


def sum_over_devices(rows):
    steps = halving_steps()
    if any(size & (size - 1) for _, _, size in steps):
        return lax.psum(rows, ("gx", "gy", "gz"))
    halvings = min(halving_count, len(steps))
    padded = jnp.pad(rows, ((0, (-rows.shape[0]) % (2**halvings)), (0, 0)))
    for axis, distance, size in steps[:halvings]:
        upper = (lax.axis_index(axis) // distance) % 2 == 1
        half = padded.shape[0] // 2
        low, high = padded[:half], padded[half:]
        keep = jnp.where(upper, high, low)
        send = jnp.where(upper, low, high)
        padded = keep + lax.ppermute(send, axis, [(i, i ^ distance) for i in range(size)])
    for axis, distance, size in steps[halvings:]:
        padded = padded + lax.ppermute(padded, axis, [(i, exchange_partner(i, distance, size)) for i in range(size)])
    for axis, distance, size in reversed(steps[:halvings]):
        upper = (lax.axis_index(axis) // distance) % 2 == 1
        other = lax.ppermute(padded, axis, [(i, i ^ distance) for i in range(size)])
        padded = jnp.where(
            upper, jnp.concatenate([other, padded]), jnp.concatenate([padded, other])
        )
    return padded[: rows.shape[0]]


def one_hot(rows, slots):
    return (jnp.arange(slots, dtype=jnp.int32)[:, None] == rows[None, :]).astype(jnp.float32)


def per_device(
    scalars,
    vectors,
    positions,
    species,
    atom_count,
    energy_weight,
    local_pairs,
    face_pairs,
    tile_counts,
    w_center,
    w_partner,
    w_radial,
    species_embed,
    w_mix,
    w_channel,
    w_read,
    w_out,
    species_energy,
):
    scalar_in = scalars[0, 0, 0]
    vector_in = vectors[0, 0, 0]
    coords = positions[0, 0, 0]
    weights_here = energy_weight[0, 0, 0]
    live_counts = tile_counts[0, 0, 0]
    local_list = local_pairs[0, 0, 0]
    face_list = face_pairs[0, 0, 0]
    channels, atom_slots = scalar_in.shape
    vector_rows = 3 * channels
    table_rows = channels + vector_rows + 3
    kind_count = species_energy.shape[0]
    local_slots = local_list.shape[1]
    face_slots = face_list.shape[2]
    species_hot = (
        species[0, 0, 0][None, :] == jnp.arange(kind_count, dtype=jnp.int32)[:, None]
    ).astype(jnp.float32)
    valid_atoms = (jnp.arange(atom_slots, dtype=jnp.int32) < atom_count[0, 0, 0]).astype(
        jnp.float32
    )

    edge_params = (w_radial, w_mix, w_channel, w_read, w_out)
    vector_flat = vector_in.reshape(vector_rows, atom_slots)
    own_table = jnp.concatenate([scalar_in, vector_flat, coords], axis=0)
    species_row = species[0, 0, 0].astype(jnp.float32)
    packet = jnp.concatenate([own_table, weights_here[None, :], species_row[None, :]], axis=0)
    arrived = [shift(packet, direction, -1) for direction in range(3)]
    far_tables = [incoming[:table_rows] for incoming in arrived]
    partner_weights = [weights_here] + [incoming[table_rows] for incoming in arrived]
    partner_species = [species_hot] + [
        (incoming[table_rows + 1][None, :] == jnp.arange(kind_count, dtype=jnp.float32)[:, None]).astype(
            jnp.float32
        )
        for incoming in arrived
    ]

    center_rows = jnp.concatenate([local_list[0]] + [face_list[d, 0] for d in range(3)])
    partner_rows = [local_list[1]] + [face_list[d, 1] for d in range(3)]
    center_hot = one_hot(center_rows, atom_slots)
    partner_hot = [one_hot(rows, atom_slots) for rows in partner_rows]
    slot_sizes = [local_slots] + [face_slots] * 3
    live_mask = jnp.concatenate(
        [
            (jnp.arange(size, dtype=jnp.int32) < live_counts[tile]).astype(jnp.float32)
            for tile, size in enumerate(slot_sizes)
        ]
    )
    offset = jnp.concatenate(
        [jnp.zeros((3, local_slots), jnp.float32)]
        + [
            jnp.broadcast_to(
                cell_edge * (jnp.arange(3) == d).astype(jnp.float32)[:, None], (3, face_slots)
            )
            for d in range(3)
        ],
        axis=1,
    )
    pair_weight = jnp.dot(weights_here, center_hot, precision=lax.Precision.HIGH) + jnp.concatenate(
        [
            jnp.dot(weight_row, hot, precision=lax.Precision.HIGH)
            for weight_row, hot in zip(partner_weights, partner_hot)
        ]
    )

    def pair_loss(center_matrix, partner_matrix, embed_table, params_in, own_in, far_in):
        def projected(matrix, embed_row, table, hot_kinds):
            proj = jnp.dot(matrix.T, table[:channels], precision=lax.Precision.HIGH) + jnp.dot(
                embed_row.T, hot_kinds, precision=highest
            )
            return jnp.concatenate([proj, table[channels:]], axis=0)

        center_in = projected(center_matrix, embed_table[0], own_in, species_hot)
        partner_in = [
            projected(partner_matrix, embed_table[1], table, hot_kinds)
            for table, hot_kinds in zip([own_in] + list(far_in), partner_species)
        ]
        center_side = jnp.dot(center_in, center_hot, precision=lax.Precision.HIGH)
        partner_side = jnp.concatenate(
            [jnp.dot(table, hot, precision=lax.Precision.HIGH) for table, hot in zip(partner_in, partner_hot)],
            axis=1,
        )
        pair_count = center_side.shape[1]
        partner_coords = jnp.concatenate(
            [
                jnp.dot(table[channels + vector_rows :], hot, precision=highest)
                for table, hot in zip(partner_in, partner_hot)
            ],
            axis=1,
        )
        center_coords = jnp.dot(center_in[channels + vector_rows :], center_hot, precision=highest)
        displace = partner_coords + offset - center_coords
        energies = edge_energy(
            params_in,
            center_side[:channels],
            partner_side[:channels],
            center_side[channels : channels + vector_rows].reshape(3, channels, pair_count),
            partner_side[channels : channels + vector_rows].reshape(3, channels, pair_count),
            displace,
        )
        halves = 0.5 * live_mask * energies
        return jnp.sum(halves * pair_weight), halves

    weighted_sum, pull_back, halves = jax.vjp(
        pair_loss, w_center, w_partner, species_embed, edge_params, own_table, far_tables,
        has_aux=True,
    )
    center_matrix_grad, partner_matrix_grad, embed_grad, param_grad, own_grad, far_grad = pull_back(
        jnp.ones_like(weighted_sum)
    )
    center_energy = jnp.dot(center_hot, halves, precision=lax.Precision.HIGH)
    starts = [0, local_slots] + [local_slots + face_slots * (d + 1) for d in range(3)]
    partner_energy = [
        jnp.dot(hot, halves[starts[tile] : starts[tile + 1]], precision=lax.Precision.HIGH)
        for tile, hot in enumerate(partner_hot)
    ]

    returned = [
        shift(jnp.concatenate([far_grad[d], partner_energy[d + 1][None, :]], axis=0), d, 1)
        for d in range(3)
    ]
    table_grad = own_grad
    for back_in in returned:
        table_grad = table_grad + back_in[:table_rows]
    pair_energy = center_energy + partner_energy[0]
    for back_in in returned:
        pair_energy = pair_energy + back_in[table_rows]
    scalar_grad = table_grad[:channels]
    vector_grad = table_grad[channels : channels + vector_rows].reshape(3, channels, atom_slots)
    coord_grad = table_grad[channels + vector_rows :]

    self_energy = valid_atoms * jnp.dot(species_energy, species_hot, precision=lax.Precision.HIGH)
    reference_grad = jnp.dot(species_hot, weights_here * valid_atoms, precision=lax.Precision.HIGH)
    lanes = channels

    def as_rows(piece):
        flat = piece.reshape(-1)
        return jnp.pad(flat, (0, (-flat.shape[0]) % lanes)).reshape(-1, lanes)

    grad_pieces = [
        center_matrix_grad,
        partner_matrix_grad,
        param_grad[0],
        embed_grad,
        param_grad[1],
        param_grad[2],
        param_grad[3],
    ]
    tail = jnp.concatenate([param_grad[4].reshape(-1), reference_grad])
    sizes = [piece.size for piece in grad_pieces] + [tail.shape[0]]
    local_rows = jnp.concatenate([as_rows(piece) for piece in grad_pieces] + [as_rows(tail)], axis=0)
    domain_total = lax.axis_size("gx") * lax.axis_size("gy") * lax.axis_size("gz")
    summed = sum_over_devices(local_rows) / domain_total
    weight_grad = summed.reshape(-1)[: sum(sizes)]
    atom_energy = self_energy + pair_energy
    return (
        atom_energy[None, None, None],
        coord_grad[None, None, None],
        scalar_grad[None, None, None],
        vector_grad[None, None, None],
        weight_grad,
    )


def solution(mesh):
    return jax.shard_map(
        per_device,
        mesh=mesh,
        in_specs=(
            P("gx", "gy", "gz", None, None),
            P("gx", "gy", "gz", None, None, None),
            P("gx", "gy", "gz", None, None),
            P("gx", "gy", "gz", None),
            P("gx", "gy", "gz"),
            P("gx", "gy", "gz", None),
            P("gx", "gy", "gz", None, None),
            P("gx", "gy", "gz", None, None, None),
            P("gx", "gy", "gz", None),
            P(),
            P(),
            P(),
            P(),
            P(),
            P(),
            P(),
            P(),
            P(),
        ),
        out_specs=(
            P("gx", "gy", "gz", None),
            P("gx", "gy", "gz", None, None),
            P("gx", "gy", "gz", None, None),
            P("gx", "gy", "gz", None, None, None),
            P(),
        ),
        check_vma=False,
    )
```

```python
import jax
import jax.numpy as jnp
from jax import lax
from jax.sharding import PartitionSpec as P

cutoff_radius = 5.0
cell_edge = 6.0
highest = lax.Precision.HIGHEST
halving_count = 3


def from_behind(block, axis, distance):
    devices = range(lax.axis_size(axis))
    route = [((i - distance) % len(devices), i) for i in devices]
    return lax.ppermute(block, axis, route)


def edge_energy(edge_params, center_proj, partner_proj, center_vecs, partner_vecs, displace):
    radial_weight, mix_weight, channel_weight, read_weight, out_weight = edge_params
    squared = jnp.sum(displace * displace, axis=0)
    basis_count = radial_weight.shape[0]
    spacing = cutoff_radius * cutoff_radius / (basis_count - 1)
    centers_sq = spacing * jnp.arange(basis_count).astype(jnp.float32)
    radial_basis = jnp.exp(-jnp.square((squared[None, :] - centers_sq[:, None]) / spacing))
    latent_in = (
        center_proj + partner_proj + jnp.dot(radial_weight.T, radial_basis, precision=lax.Precision.HIGH)
    )
    first_hidden = jax.nn.silu(latent_in)
    second = first_hidden + jax.nn.silu(jnp.dot(mix_weight.T, first_hidden, precision=lax.Precision.HIGH))
    vector_gain = jnp.dot(channel_weight[0].T, second, precision=lax.Precision.HIGH)
    tensor_gain = jnp.dot(channel_weight[1].T, second, precision=lax.Precision.HIGH)
    bond_vector = displace / cutoff_radius
    along_partner = jnp.sum(bond_vector[:, None, :] * partner_vecs, axis=0)
    along_center = jnp.sum(bond_vector[:, None, :] * center_vecs, axis=0)
    inner_product = jnp.sum(center_vecs * partner_vecs, axis=0)
    scaled_sq = squared / (cutoff_radius * cutoff_radius)
    quadratic = along_center * along_partner - scaled_sq[None, :] * inner_product / 3.0
    mixed_latent = second + vector_gain * along_partner + tensor_gain * quadratic
    readout = jnp.dot(
        out_weight,
        jax.nn.silu(jnp.dot(read_weight.T, mixed_latent, precision=lax.Precision.HIGH)),
        precision=highest,
    )
    envelope = 1.0 / (1.0 + scaled_sq)
    return envelope * readout


def shift(payload, direction, distance):
    return from_behind(payload, ("gx", "gy", "gz")[direction], distance)


def halving_steps():
    steps = []
    for axis in ("gx", "gz", "gy"):
        size = lax.axis_size(axis)
        distance = 1
        while distance < size:
            steps.append((axis, distance, size))
            distance *= 2
    return steps


def exchange_partner(index, distance, size):
    if distance >= 2 and 2 * distance == size:
        unit = distance // 2
        digit, low = divmod(index, unit)
        return (3 - digit) * unit + low
    return index ^ distance


def halving_order(steps):
    ordered = list(steps)
    for k in range(len(ordered) - 1):
        axis, distance, size = ordered[k + 1]
        if ordered[k] == (axis, distance // 2, size) and distance >= 4 and 2 * distance == size:
            ordered[k], ordered[k + 1] = ordered[k + 1], ordered[k]
    return ordered


def sum_over_devices(rows):
    steps = halving_steps()
    if any(size & (size - 1) for _, _, size in steps):
        return lax.psum(rows, ("gx", "gy", "gz"))
    halvings = min(halving_count, len(steps))
    padded = jnp.pad(rows, ((0, (-rows.shape[0]) % (2**halvings)), (0, 0)))
    halving = halving_order(steps[:halvings])
    for axis, distance, size in halving:
        upper = (lax.axis_index(axis) // distance) % 2 == 1
        half = padded.shape[0] // 2
        low, high = padded[:half], padded[half:]
        keep = jnp.where(upper, high, low)
        send = jnp.where(upper, low, high)
        padded = keep + lax.ppermute(send, axis, [(i, exchange_partner(i, distance, size)) for i in range(size)])
    for axis, distance, size in steps[halvings:]:
        padded = padded + lax.ppermute(padded, axis, [(i, exchange_partner(i, distance, size)) for i in range(size)])
    for axis, distance, size in reversed(halving):
        upper = (lax.axis_index(axis) // distance) % 2 == 1
        other = lax.ppermute(padded, axis, [(i, exchange_partner(i, distance, size)) for i in range(size)])
        padded = jnp.where(
            upper, jnp.concatenate([other, padded]), jnp.concatenate([padded, other])
        )
    return padded[: rows.shape[0]]


def one_hot(rows, slots):
    return (jnp.arange(slots, dtype=jnp.int32)[:, None] == rows[None, :]).astype(jnp.float32)


def per_device(
    scalars,
    vectors,
    positions,
    species,
    atom_count,
    energy_weight,
    local_pairs,
    face_pairs,
    tile_counts,
    w_center,
    w_partner,
    w_radial,
    species_embed,
    w_mix,
    w_channel,
    w_read,
    w_out,
    species_energy,
):
    scalar_in = scalars[0, 0, 0]
    vector_in = vectors[0, 0, 0]
    coords = positions[0, 0, 0]
    weights_here = energy_weight[0, 0, 0]
    live_counts = tile_counts[0, 0, 0]
    local_list = local_pairs[0, 0, 0]
    face_list = face_pairs[0, 0, 0]
    channels, atom_slots = scalar_in.shape
    vector_rows = 3 * channels
    table_rows = channels + vector_rows + 3
    kind_count = species_energy.shape[0]
    local_slots = local_list.shape[1]
    face_slots = face_list.shape[2]
    species_hot = (
        species[0, 0, 0][None, :] == jnp.arange(kind_count, dtype=jnp.int32)[:, None]
    ).astype(jnp.float32)
    valid_atoms = (jnp.arange(atom_slots, dtype=jnp.int32) < atom_count[0, 0, 0]).astype(
        jnp.float32
    )

    edge_params = (w_radial, w_mix, w_channel, w_read, w_out)
    vector_flat = vector_in.reshape(vector_rows, atom_slots)
    own_table = jnp.concatenate([scalar_in, vector_flat, coords], axis=0)
    species_row = species[0, 0, 0].astype(jnp.float32)
    packet = jnp.concatenate([own_table, weights_here[None, :], species_row[None, :]], axis=0)
    arrived = [shift(packet, direction, -1) for direction in range(3)]
    far_tables = [incoming[:table_rows] for incoming in arrived]
    partner_weights = [weights_here] + [incoming[table_rows] for incoming in arrived]
    partner_species = [species_hot] + [
        (incoming[table_rows + 1][None, :] == jnp.arange(kind_count, dtype=jnp.float32)[:, None]).astype(
            jnp.float32
        )
        for incoming in arrived
    ]

    center_rows = jnp.concatenate([local_list[0]] + [face_list[d, 0] for d in range(3)])
    partner_rows = [local_list[1]] + [face_list[d, 1] for d in range(3)]
    center_hot = one_hot(center_rows, atom_slots)
    partner_hot = [one_hot(rows, atom_slots) for rows in partner_rows]
    slot_sizes = [local_slots] + [face_slots] * 3
    live_mask = jnp.concatenate(
        [
            (jnp.arange(size, dtype=jnp.int32) < live_counts[tile]).astype(jnp.float32)
            for tile, size in enumerate(slot_sizes)
        ]
    )
    offset = jnp.concatenate(
        [jnp.zeros((3, local_slots), jnp.float32)]
        + [
            jnp.broadcast_to(
                cell_edge * (jnp.arange(3) == d).astype(jnp.float32)[:, None], (3, face_slots)
            )
            for d in range(3)
        ],
        axis=1,
    )
    pair_weight = jnp.dot(weights_here, center_hot, precision=lax.Precision.HIGH) + jnp.concatenate(
        [
            jnp.dot(weight_row, hot, precision=lax.Precision.HIGH)
            for weight_row, hot in zip(partner_weights, partner_hot)
        ]
    )

    def pair_loss(center_matrix, partner_matrix, embed_table, params_in, own_in, far_in):
        def projected(matrix, embed_row, table, hot_kinds):
            proj = jnp.dot(matrix.T, table[:channels], precision=lax.Precision.HIGH) + jnp.dot(
                embed_row.T, hot_kinds, precision=highest
            )
            return jnp.concatenate([proj, table[channels:]], axis=0)

        center_in = projected(center_matrix, embed_table[0], own_in, species_hot)
        partner_in = [
            projected(partner_matrix, embed_table[1], table, hot_kinds)
            for table, hot_kinds in zip([own_in] + list(far_in), partner_species)
        ]
        center_side = jnp.dot(center_in, center_hot, precision=lax.Precision.HIGH)
        partner_side = jnp.concatenate(
            [jnp.dot(table, hot, precision=lax.Precision.HIGH) for table, hot in zip(partner_in, partner_hot)],
            axis=1,
        )
        pair_count = center_side.shape[1]
        partner_coords = jnp.concatenate(
            [
                jnp.dot(table[channels + vector_rows :], hot, precision=highest)
                for table, hot in zip(partner_in, partner_hot)
            ],
            axis=1,
        )
        center_coords = jnp.dot(center_in[channels + vector_rows :], center_hot, precision=highest)
        displace = partner_coords + offset - center_coords
        energies = edge_energy(
            params_in,
            center_side[:channels],
            partner_side[:channels],
            center_side[channels : channels + vector_rows].reshape(3, channels, pair_count),
            partner_side[channels : channels + vector_rows].reshape(3, channels, pair_count),
            displace,
        )
        halves = 0.5 * live_mask * energies
        return jnp.sum(halves * pair_weight), halves

    weighted_sum, pull_back, halves = jax.vjp(
        pair_loss, w_center, w_partner, species_embed, edge_params, own_table, far_tables,
        has_aux=True,
    )
    center_matrix_grad, partner_matrix_grad, embed_grad, param_grad, own_grad, far_grad = pull_back(
        jnp.ones_like(weighted_sum)
    )
    center_energy = jnp.dot(center_hot, halves, precision=lax.Precision.HIGH)
    starts = [0, local_slots] + [local_slots + face_slots * (d + 1) for d in range(3)]
    partner_energy = [
        jnp.dot(hot, halves[starts[tile] : starts[tile + 1]], precision=lax.Precision.HIGH)
        for tile, hot in enumerate(partner_hot)
    ]

    returned = [
        shift(jnp.concatenate([far_grad[d], partner_energy[d + 1][None, :]], axis=0), d, 1)
        for d in range(3)
    ]
    table_grad = own_grad
    for back_in in returned:
        table_grad = table_grad + back_in[:table_rows]
    pair_energy = center_energy + partner_energy[0]
    for back_in in returned:
        pair_energy = pair_energy + back_in[table_rows]
    scalar_grad = table_grad[:channels]
    vector_grad = table_grad[channels : channels + vector_rows].reshape(3, channels, atom_slots)
    coord_grad = table_grad[channels + vector_rows :]

    self_energy = valid_atoms * jnp.dot(species_energy, species_hot, precision=lax.Precision.HIGH)
    reference_grad = jnp.dot(species_hot, weights_here * valid_atoms, precision=lax.Precision.HIGH)
    lanes = channels

    def as_rows(piece):
        flat = piece.reshape(-1)
        return jnp.pad(flat, (0, (-flat.shape[0]) % lanes)).reshape(-1, lanes)

    grad_pieces = [
        center_matrix_grad,
        partner_matrix_grad,
        param_grad[0],
        embed_grad,
        param_grad[1],
        param_grad[2],
        param_grad[3],
    ]
    tail = jnp.concatenate([param_grad[4].reshape(-1), reference_grad])
    sizes = [piece.size for piece in grad_pieces] + [tail.shape[0]]
    local_rows = jnp.concatenate([as_rows(piece) for piece in grad_pieces] + [as_rows(tail)], axis=0)
    domain_total = lax.axis_size("gx") * lax.axis_size("gy") * lax.axis_size("gz")
    summed = sum_over_devices(local_rows) / domain_total
    weight_grad = summed.reshape(-1)[: sum(sizes)]
    atom_energy = self_energy + pair_energy
    return (
        atom_energy[None, None, None],
        coord_grad[None, None, None],
        scalar_grad[None, None, None],
        vector_grad[None, None, None],
        weight_grad,
    )


def solution(mesh):
    return jax.shard_map(
        per_device,
        mesh=mesh,
        in_specs=(
            P("gx", "gy", "gz", None, None),
            P("gx", "gy", "gz", None, None, None),
            P("gx", "gy", "gz", None, None),
            P("gx", "gy", "gz", None),
            P("gx", "gy", "gz"),
            P("gx", "gy", "gz", None),
            P("gx", "gy", "gz", None, None),
            P("gx", "gy", "gz", None, None, None),
            P("gx", "gy", "gz", None),
            P(),
            P(),
            P(),
            P(),
            P(),
            P(),
            P(),
            P(),
            P(),
        ),
        out_specs=(
            P("gx", "gy", "gz", None),
            P("gx", "gy", "gz", None, None),
            P("gx", "gy", "gz", None, None),
            P("gx", "gy", "gz", None, None, None),
            P(),
        ),
        check_vma=False,
    )
```
